256 devices in a mesh: pipe: 8 (over z_hi, core), tensor: 8 (over z_lo, y), dp: 4 (over x).
Axes of the slice: x: 4, y: 4, z: 8 (z_hi: 4, z_lo: 2; z = z_hi * 2 + z_lo), core: 2. Of those that a mesh axis runs over, the one named last changes fastest.
Arguments:
- queries: bfloat16 [8, 4, 1024, 6144], P('pipe', 'dp', None, 'tensor'), may hold values from -128 to 128
- key_heads: bfloat16 [8, 4, 1024, 6144], P('pipe', 'dp', None, 'tensor'), may hold values from -6 to 6
- value_heads: bfloat16 [8, 4, 1024, 6144], P('pipe', 'dp', None, 'tensor'), may hold values from -6 to 6
- context_grad: bfloat16 [8, 4, 1024, 6144], P('pipe', 'dp', None, 'tensor'), may hold values from -6 to 6
- output_grad: bfloat16 [8, 4, 1024, 6144], P('pipe', 'dp', 'tensor'), may hold values from -6 to 6
- random_blocks: int32 [48, 14, 3], P('tensor'), may hold values from 1 to 14, as said below
Outputs:
- query_grad: bfloat16 [8, 4, 1024, 6144], P('pipe', 'dp', None, 'tensor')
- key_grad: bfloat16 [8, 4, 1024, 6144], P('pipe', 'dp', None, 'tensor')
- value_grad: bfloat16 [8, 4, 1024, 6144], P('pipe', 'dp', None, 'tensor')
- weight_grad: bfloat16 [8, 3072, 6144], P('pipe', 'dp', 'tensor')
The draws below stay inside these ranges and needn't reach their ends.
Inputs may be any that keep to these rules, and one draw needn't show every extreme that they name: `random_blocks`: in row r (query block r + 1) the 3 entries are distinct, none is 0 or 16 - 1, and none lies within one block of r + 1.
All inputs are finite; a program needn't handle non-finite values.
Results may differ from the reference program's by a relative error of at most 0.029.
Values may be sent and summed in bfloat16 or wider, within the bound.
No kernel may reach another device: no remote copies, remote signals or barrier semaphores. Data moves between devices by JAX's collectives and lax.ppermute only.
A program may use at most 256 MiB of HBM per device.

```python
import math
from functools import partial
import jax
import jax.numpy as jnp
from jax import lax

HEADS = 48
HD = 128
DW = 6144
BLK = 64
R = 3
S = 1024
N_PIPE = 8
N_DP = 4


def query_key_pair(key):
    base_key = jax.random.fold_in(key, 7)
    first_key, second_key = jax.random.split(base_key)
    full_shape = (N_PIPE, N_DP, S, HEADS * HD)
    keys_drawn = jax.random.normal(first_key, full_shape, jnp.float32)
    queries_drawn = jax.random.normal(second_key, full_shape, jnp.float32)
    keys_drawn = jnp.clip(keys_drawn, -6.0, 6.0)
    queries_drawn = jnp.clip(queries_drawn, -6.0, 6.0)
    return (queries_drawn, keys_drawn)


def draw_queries(key, part):
    return query_key_pair(key)[0].astype(jnp.bfloat16)


def draw_key_heads(key, part):
    return query_key_pair(key)[1].astype(jnp.bfloat16)


def draw_random_blocks(key, part):
    blocks = S // BLK
    ranks = jax.random.randint(jax.random.fold_in(key, 3), (HEADS, blocks - 2, blocks), 0, 1 << 20, dtype=jnp.int32)
    ranks = ranks * blocks + jnp.arange(blocks, dtype=jnp.int32)
    query_block = jnp.arange(1, blocks - 1, dtype=jnp.int32)[:, None]
    key_block = jnp.arange(blocks, dtype=jnp.int32)[None, :]
    barred = (key_block == 0) | (key_block == blocks - 1) | (jnp.abs(key_block - query_block) <= 1)
    ranks = jnp.where(barred[None], -1, ranks)
    chosen = lax.top_k(ranks, R)[1]
    return chosen.astype(jnp.int32)


def level_of(own_key, dims, cuts, smallest, high):
    loudness = 1.0
    for dim, parts in cuts:
        heights = jax.random.uniform(jax.random.fold_in(jax.random.fold_in(own_key, 6), dim), (parts,), jnp.float32, smallest / len(cuts), high / len(cuts))
        loudness = loudness * jnp.repeat(jnp.exp(heights), dims[dim] // parts).reshape((-1,) + (1,) * (len(dims) - 1 - dim))
    return loudness


def gaussian(stream_key, extent, scale, reach, cuts=(), held_as=jnp.bfloat16):
    drawn = scale * jax.random.normal(stream_key, extent, jnp.float32)
    if cuts:
        drawn = drawn * level_of(stream_key, extent, cuts, -0.22, 0.18)
    return jnp.clip(drawn, -reach, reach).astype(held_as)


def setup_inputs(seed: int = 0) -> dict:
    seeds = jax.random.split(jax.random.key(seed), 7)
    return {
        "queries": draw_queries(jax.random.fold_in(seeds[6], 71), 0),
        "key_heads": draw_key_heads(jax.random.fold_in(seeds[6], 71), 0),
        "value_heads": gaussian(seeds[2], (N_PIPE, N_DP, S, HEADS * HD), 1.0, 6.0, ((0, 8), (1, 4), (3, 8))),
        "context_grad": gaussian(seeds[3], (N_PIPE, N_DP, S, HEADS * HD), 1.0, 6.0, ((0, 8), (1, 4), (3, 8))),
        "output_grad": gaussian(seeds[4], (N_PIPE, N_DP, S, DW), 1.0, 6.0, ((0, 8), (1, 4), (2, 8))),
        "random_blocks": draw_random_blocks(jax.random.fold_in(seeds[6], 71), 0),
    }


def allowed_blocks(random_rows):
    blocks = random_rows.shape[0] + 2
    query_block = jnp.arange(blocks, dtype=jnp.int32)[:, None]
    key_block = jnp.arange(blocks, dtype=jnp.int32)[None, :]
    random_hit = jnp.any(random_rows[:, :, None] == jnp.arange(blocks, dtype=jnp.int32)[None, None, :], axis=1)
    empty_row = jnp.zeros((1, blocks), dtype=jnp.bool_)
    random_hit = jnp.concatenate([empty_row, random_hit, empty_row], axis=0)
    global_hit = (query_block == 0) | (query_block == blocks - 1) | (key_block == 0) | (key_block == blocks - 1)
    return global_hit | (jnp.abs(query_block - key_block) <= 1) | random_hit

def microbatch_backward(inputs, allowed):
    queries, key_heads, value_heads, context_grad = inputs
    score_scale = 1.0 / math.sqrt(HD)
    query_f = queries.reshape(S, HEADS, HD).astype(jnp.float32)
    key_f = key_heads.reshape(S, HEADS, HD).astype(jnp.float32)
    value_f = value_heads.reshape(S, HEADS, HD).astype(jnp.float32)
    grad_f = context_grad.reshape(S, HEADS, HD).astype(jnp.float32)
    scores = jnp.einsum('shd,thd->hst', query_f, key_f) * score_scale
    scores = jnp.where(allowed, scores, -1e+30)
    row_peak = lax.optimization_barrier(jnp.max(scores, axis=-1, keepdims=True))
    raised = jnp.exp(scores - row_peak)
    prob_full = raised / lax.optimization_barrier(jnp.sum(raised, axis=-1, keepdims=True))
    prob_round = lax.optimization_barrier(prob_full.astype(jnp.bfloat16)).astype(jnp.float32)
    context = jnp.einsum('hst,thd->shd', prob_round, value_f).astype(jnp.bfloat16)
    context_f = lax.optimization_barrier(context).astype(jnp.float32)
    prob_grad = jnp.einsum('shd,thd->hst', grad_f, value_f)
    row_dot = jnp.einsum('shd,shd->hs', grad_f, context_f)
    score_grad = prob_full * (prob_grad - row_dot[:, :, None])
    score_round = lax.optimization_barrier(score_grad.astype(jnp.bfloat16)).astype(jnp.float32)
    query_grad = (jnp.einsum('hst,thd->shd', score_round, key_f) * score_scale).astype(jnp.bfloat16)
    key_grad = (jnp.einsum('hst,shd->thd', score_round, query_f) * score_scale).astype(jnp.bfloat16)
    value_grad = jnp.einsum('hst,shd->thd', prob_round, grad_f).astype(jnp.bfloat16)
    width_all = HEADS * HD
    return (query_grad.reshape(S, width_all), key_grad.reshape(S, width_all), value_grad.reshape(S, width_all), context.reshape(S, width_all))

def layer_sum(pair):
    grad_rows, ctx_rows = pair
    return lax.dot_general(grad_rows.astype(jnp.float32), ctx_rows.astype(jnp.float32), (((0,), (0,)), ((), ()))).astype(jnp.bfloat16)

def reference(queries, key_heads, value_heads, context_grad, output_grad, random_blocks):
    per_head = jax.vmap(allowed_blocks)(random_blocks)
    allowed = jnp.repeat(jnp.repeat(per_head, BLK, axis=1), BLK, axis=2)
    micro_count = N_PIPE * N_DP
    width_all = HEADS * HD
    flat_inputs = (queries.reshape(micro_count, S, width_all), key_heads.reshape(micro_count, S, width_all), value_heads.reshape(micro_count, S, width_all), context_grad.reshape(micro_count, S, width_all))
    results = lax.map(partial(microbatch_backward, allowed=allowed), flat_inputs)
    full_shape = (N_PIPE, N_DP, S, width_all)
    query_grad = results[0].reshape(full_shape)
    key_grad = results[1].reshape(full_shape)
    value_grad = results[2].reshape(full_shape)
    contexts = results[3].reshape(N_PIPE, N_DP * S, width_all)
    tokens_grad = output_grad.reshape(N_PIPE, N_DP * S, DW)
    layer_grad = lax.map(layer_sum, (tokens_grad, contexts))
    half_rows = DW // 2
    pieces = []
    for section in range(N_PIPE):
        upper_half = 1 if section >= N_PIPE // 2 else 0
        first_row = upper_half * half_rows
        rows_own = layer_grad[section, first_row:first_row + half_rows].astype(jnp.float32)
        rows_twin = layer_grad[N_PIPE - 1 - section, first_row:first_row + half_rows].astype(jnp.float32)
        pieces.append((rows_own + rows_twin).astype(jnp.bfloat16))
    weight_grad = jnp.stack(pieces)
    return (query_grad, key_grad, value_grad, weight_grad)
```

```python
import functools
import math

import jax
import jax.numpy as jnp
from jax import lax
from jax.experimental import pallas as pl
from jax.experimental.pallas import tpu as pltpu
from jax.sharding import PartitionSpec as P

BLK = 64
ROWS = 256


def attention_kernel(
    blocks, head_size, rb_ref, q_ref, k_ref, v_ref, g_ref, dq_ref, ctx_ref, dk_ref, dv_ref,
    dk_acc, dv_acc,
):
    head = pl.program_id(0)
    chunk = pl.program_id(1)
    score_scale = 1.0 / math.sqrt(head_size)
    tokens = k_ref.shape[0]
    per_chunk = q_ref.shape[0] // BLK
    mids = blocks - 2

    @pl.when(chunk == 0)
    def _():
        dk_acc[...] = jnp.zeros_like(dk_acc)
        dv_acc[...] = jnp.zeros_like(dv_acc)

    q = q_ref[...]
    k = k_ref[...]
    v = v_ref[...]
    g = g_ref[...]
    scores = lax.dot_general(
        q, k, (((1,), (1,)), ((), ())), preferred_element_type=jnp.float32
    ) * score_scale
    key_block = lax.broadcasted_iota(jnp.int32, (1, tokens), 1) // BLK
    bias_rows = []
    for i in range(per_chunk):
        qb = chunk * per_chunk + i
        row = jnp.clip(qb - 1, 0, mids - 1)
        base = (head * mids + row) * 3
        r1 = rb_ref[base]
        r2 = rb_ref[base + 1]
        r3 = rb_ref[base + 2]
        edge = jnp.logical_or(qb == 0, qb == blocks - 1)
        near = jnp.abs(key_block - qb) <= 1
        allowed = (
            (key_block == 0)
            | (key_block == blocks - 1)
            | near
            | (key_block == r1)
            | (key_block == r2)
            | (key_block == r3)
            | edge
        )
        bias = jnp.where(allowed, 0.0, -1e30).astype(jnp.float32)
        bias_rows.append(jnp.broadcast_to(bias, (BLK, tokens)))
    scores = scores + jnp.concatenate(bias_rows, axis=0)
    row_peak = jnp.max(scores, axis=1, keepdims=True)
    raised = jnp.exp(scores - row_peak)
    prob = raised / jnp.sum(raised, axis=1, keepdims=True)
    prob_b = prob.astype(jnp.bfloat16)
    ctx = jnp.dot(prob_b, v, preferred_element_type=jnp.float32).astype(jnp.bfloat16)
    ctx_ref[...] = ctx
    dprob = lax.dot_general(
        g, v, (((1,), (1,)), ((), ())), preferred_element_type=jnp.float32
    )
    row_dot = jnp.sum(
        g.astype(jnp.float32) * ctx.astype(jnp.float32), axis=1, keepdims=True
    )
    dscore = (prob * (dprob - row_dot)).astype(jnp.bfloat16)
    dq = jnp.dot(dscore, k, preferred_element_type=jnp.float32) * score_scale
    dq_ref[...] = dq.astype(jnp.bfloat16)
    dk_acc[...] += lax.dot_general(
        dscore, q, (((0,), (0,)), ((), ())), preferred_element_type=jnp.float32
    )
    dv_acc[...] += lax.dot_general(
        prob_b, g, (((0,), (0,)), ((), ())), preferred_element_type=jnp.float32
    )

    @pl.when(chunk == pl.num_programs(1) - 1)
    def _():
        dk_ref[...] = (dk_acc[...] * score_scale).astype(jnp.bfloat16)
        dv_ref[...] = dv_acc[...].astype(jnp.bfloat16)


def attention_backward(queries, key_heads, value_heads, context_grad, random_blocks):
    heads_here = random_blocks.shape[0]
    tokens, width_here = queries.shape
    head_size = width_here // heads_here
    blocks = tokens // BLK
    chunks = tokens // ROWS
    rb_flat = random_blocks.reshape(-1)
    row_spec = pl.BlockSpec((ROWS, head_size), lambda h, c, rb: (c, h))
    full_spec = pl.BlockSpec((tokens, head_size), lambda h, c, rb: (0, h))
    out_shape = jax.ShapeDtypeStruct((tokens, width_here), jnp.bfloat16)
    flops = 2 * tokens * tokens * head_size * 6 * heads_here
    call = pl.pallas_call(
        functools.partial(attention_kernel, blocks, head_size),
        out_shape=(out_shape, out_shape, out_shape, out_shape),
        grid_spec=pltpu.PrefetchScalarGridSpec(
            num_scalar_prefetch=1,
            grid=(heads_here, chunks),
            in_specs=[row_spec, full_spec, full_spec, row_spec],
            out_specs=[row_spec, row_spec, full_spec, full_spec],
            scratch_shapes=[
                pltpu.VMEM((tokens, head_size), jnp.float32),
                pltpu.VMEM((tokens, head_size), jnp.float32),
            ],
        ),
        compiler_params=pltpu.CompilerParams(
            dimension_semantics=("arbitrary", "arbitrary"),
            vmem_limit_bytes=48 * 1024 * 1024,
        ),
        cost_estimate=pl.CostEstimate(
            flops=flops,
            transcendentals=tokens * tokens * heads_here,
            bytes_accessed=7 * tokens * width_here * 2,
        ),
    )
    query_grad, context, key_grad, value_grad = call(
        rb_flat, queries, key_heads, value_heads, context_grad
    )
    return query_grad, key_grad, value_grad, context


def shift_over(block, axis, shift):
    count = lax.axis_size(axis)
    return lax.ppermute(block, axis, [(i, (i + shift) % count) for i in range(count)])


def on_device(queries, key_heads, value_heads, context_grad, output_grad, random_blocks):
    dp_count = lax.axis_size("dp")
    dp_pos = lax.axis_index("dp")
    rows_here = output_grad.shape[2]
    width_model = output_grad.shape[3]
    quarter = width_model // (2 * dp_count)
    pieces = output_grad[0, 0].reshape(rows_here, 2, dp_count, quarter).transpose(2, 0, 1, 3)
    received = [None] * dp_count
    received_own = lax.dynamic_index_in_dim(pieces, dp_pos, 0, keepdims=False)
    for shift in range(1, dp_count):
        target = (dp_pos + shift) % dp_count
        outgoing = lax.dynamic_index_in_dim(pieces, target, 0, keepdims=False)
        received[shift] = shift_over(outgoing, "dp", shift)
    received[0] = received_own
    moved_cols = jnp.stack(received)
    columns = lax.all_gather(moved_cols, "tensor", axis=1, tiled=True)

    query_grad, key_grad, value_grad, ctx_rows = attention_backward(
        queries[0, 0], key_heads[0, 0], value_heads[0, 0], context_grad[0, 0], random_blocks
    )
    tokens_all, width_here = ctx_rows.shape
    ctx_parts = [None] * dp_count
    ctx_parts[0] = ctx_rows
    for shift in range(1, dp_count):
        ctx_parts[shift] = shift_over(ctx_rows, "dp", shift)
    contexts = jnp.stack(ctx_parts)

    summed = lax.dot_general(
        columns.reshape(dp_count * tokens_all, 2 * quarter),
        contexts.reshape(dp_count * tokens_all, width_here),
        (((0,), (0,)), ((), ())),
        preferred_element_type=jnp.float32,
    ).reshape(2, quarter, width_here)
    summed_b = summed.astype(jnp.bfloat16)
    pipe_count = lax.axis_size("pipe")
    pipe_pos = lax.axis_index("pipe")
    upper_half = (pipe_pos >= pipe_count // 2).astype(jnp.int32)
    own_half = lax.dynamic_index_in_dim(summed_b, upper_half, 0, keepdims=False)
    outgoing = lax.dynamic_index_in_dim(summed_b, 1 - upper_half, 0, keepdims=False)
    incoming = lax.ppermute(
        outgoing, "pipe", [(i, pipe_count - 1 - i) for i in range(pipe_count)]
    )
    weight_grad = (own_half.astype(jnp.float32) + incoming.astype(jnp.float32)).astype(
        jnp.bfloat16
    )[None]
    shape4 = queries.shape
    return (
        query_grad.reshape(shape4),
        key_grad.reshape(shape4),
        value_grad.reshape(shape4),
        weight_grad,
    )


def solution(mesh):
    in_specs = (
        P("pipe", "dp", None, "tensor"),
        P("pipe", "dp", None, "tensor"),
        P("pipe", "dp", None, "tensor"),
        P("pipe", "dp", None, "tensor"),
        P("pipe", "dp", "tensor", None),
        P("tensor", None, None),
    )
    out_specs = (
        P("pipe", "dp", None, "tensor"),
        P("pipe", "dp", None, "tensor"),
        P("pipe", "dp", None, "tensor"),
        P("pipe", "dp", "tensor"),
    )
    return jax.shard_map(
        on_device, mesh=mesh, in_specs=in_specs, out_specs=out_specs, check_vma=False
    )
```

```python
import functools
import math

import jax
import jax.numpy as jnp
from jax import lax
from jax.experimental import pallas as pl
from jax.experimental.pallas import tpu as pltpu
from jax.sharding import PartitionSpec as P

BLK = 64
ROWS = 256


def attention_kernel(
    blocks, head_size, rb_ref, q_ref, k_ref, v_ref, g_ref, dq_ref, ctx_ref, dk_ref, dv_ref,
    dk_acc, dv_acc,
):
    head = pl.program_id(0)
    chunk = pl.program_id(1)
    score_scale = 1.0 / math.sqrt(head_size)
    tokens = k_ref.shape[0]
    per_chunk = q_ref.shape[0] // BLK
    mids = blocks - 2

    @pl.when(chunk == 0)
    def _():
        dk_acc[...] = jnp.zeros_like(dk_acc)
        dv_acc[...] = jnp.zeros_like(dv_acc)

    q = q_ref[...]
    k = k_ref[...]
    v = v_ref[...]
    g = g_ref[...]
    scores = lax.dot_general(
        q, k, (((1,), (1,)), ((), ())), preferred_element_type=jnp.float32
    ) * score_scale
    key_block = lax.broadcasted_iota(jnp.int32, (1, tokens), 1) // BLK
    bias_rows = []
    for i in range(per_chunk):
        qb = chunk * per_chunk + i
        row = jnp.clip(qb - 1, 0, mids - 1)
        base = (head * mids + row) * 3
        r1 = rb_ref[base]
        r2 = rb_ref[base + 1]
        r3 = rb_ref[base + 2]
        edge = jnp.logical_or(qb == 0, qb == blocks - 1)
        near = jnp.abs(key_block - qb) <= 1
        allowed = (
            (key_block == 0)
            | (key_block == blocks - 1)
            | near
            | (key_block == r1)
            | (key_block == r2)
            | (key_block == r3)
            | edge
        )
        bias = jnp.where(allowed, 0.0, -1e30).astype(jnp.float32)
        bias_rows.append(jnp.broadcast_to(bias, (BLK, tokens)))
    scores = scores + jnp.concatenate(bias_rows, axis=0)
    row_peak = jnp.max(scores, axis=1, keepdims=True)
    raised = jnp.exp(scores - row_peak)
    prob = raised / jnp.sum(raised, axis=1, keepdims=True)
    prob_b = prob.astype(jnp.bfloat16)
    ctx = jnp.dot(prob_b, v, preferred_element_type=jnp.float32).astype(jnp.bfloat16)
    ctx_ref[...] = ctx
    dprob = lax.dot_general(
        g, v, (((1,), (1,)), ((), ())), preferred_element_type=jnp.float32
    )
    row_dot = jnp.sum(
        g.astype(jnp.float32) * ctx.astype(jnp.float32), axis=1, keepdims=True
    )
    dscore = (prob * (dprob - row_dot)).astype(jnp.bfloat16)
    dq = jnp.dot(dscore, k, preferred_element_type=jnp.float32) * score_scale
    dq_ref[...] = dq.astype(jnp.bfloat16)
    dk_acc[...] += lax.dot_general(
        dscore, q, (((0,), (0,)), ((), ())), preferred_element_type=jnp.float32
    )
    dv_acc[...] += lax.dot_general(
        prob_b, g, (((0,), (0,)), ((), ())), preferred_element_type=jnp.float32
    )

    @pl.when(chunk == pl.num_programs(1) - 1)
    def _():
        dk_ref[...] = (dk_acc[...] * score_scale).astype(jnp.bfloat16)
        dv_ref[...] = dv_acc[...].astype(jnp.bfloat16)


def attention_backward(queries, key_heads, value_heads, context_grad, random_blocks):
    heads_here = random_blocks.shape[0]
    tokens, width_here = queries.shape
    head_size = width_here // heads_here
    blocks = tokens // BLK
    chunks = tokens // ROWS
    rb_flat = random_blocks.reshape(-1)
    row_spec = pl.BlockSpec((ROWS, head_size), lambda h, c, rb: (c, h))
    full_spec = pl.BlockSpec((tokens, head_size), lambda h, c, rb: (0, h))
    out_shape = jax.ShapeDtypeStruct((tokens, width_here), jnp.bfloat16)
    flops = 2 * tokens * tokens * head_size * 6 * heads_here
    call = pl.pallas_call(
        functools.partial(attention_kernel, blocks, head_size),
        out_shape=(out_shape, out_shape, out_shape, out_shape),
        grid_spec=pltpu.PrefetchScalarGridSpec(
            num_scalar_prefetch=1,
            grid=(heads_here, chunks),
            in_specs=[row_spec, full_spec, full_spec, row_spec],
            out_specs=[row_spec, row_spec, full_spec, full_spec],
            scratch_shapes=[
                pltpu.VMEM((tokens, head_size), jnp.float32),
                pltpu.VMEM((tokens, head_size), jnp.float32),
            ],
        ),
        compiler_params=pltpu.CompilerParams(
            dimension_semantics=("arbitrary", "arbitrary"),
            vmem_limit_bytes=48 * 1024 * 1024,
        ),
        cost_estimate=pl.CostEstimate(
            flops=flops,
            transcendentals=tokens * tokens * heads_here,
            bytes_accessed=7 * tokens * width_here * 2,
        ),
    )
    query_grad, context, key_grad, value_grad = call(
        rb_flat, queries, key_heads, value_heads, context_grad
    )
    return query_grad, key_grad, value_grad, context


def shift_over(block, axis, shift):
    count = lax.axis_size(axis)
    return lax.ppermute(block, axis, [(i, (i + shift) % count) for i in range(count)])


def wgrad_kernel(cols_ref, own_ref, left_ref, far_lo_ref, far_hi_ref, right_ref, out_ref, acc):
    slot = pl.program_id(0)
    half = far_lo_ref.shape[0]

    def term(cols, ctx):
        return lax.dot_general(
            cols, ctx, (((0,), (0,)), ((), ())), preferred_element_type=jnp.float32
        )

    @pl.when(slot == 0)
    def _():
        acc[...] = term(cols_ref[...], own_ref[...])

    @pl.when(slot == 1)
    def _():
        acc[...] += term(cols_ref[...], left_ref[...])

    @pl.when(slot == 2)
    def _():
        acc[...] += term(cols_ref[:half, :], far_lo_ref[...]) + term(
            cols_ref[half:, :], far_hi_ref[...]
        )

    @pl.when(slot == 3)
    def _():
        out_ref[...] = (acc[...] + term(cols_ref[...], right_ref[...])).astype(out_ref.dtype)


def weight_block(cols, ctx_parts):
    slots, tokens, rows = cols.shape
    width = ctx_parts[0].shape[1]
    full = pl.BlockSpec((tokens, width), lambda s: (0, 0))
    half = pl.BlockSpec((tokens // 2, width), lambda s: (0, 0))
    return pl.pallas_call(
        wgrad_kernel,
        out_shape=jax.ShapeDtypeStruct((rows, width), jnp.bfloat16),
        grid=(slots,),
        in_specs=[
            pl.BlockSpec((None, tokens, rows), lambda s: (s, 0, 0)),
            full,
            full,
            half,
            half,
            full,
        ],
        out_specs=pl.BlockSpec((rows, width), lambda s: (0, 0)),
        scratch_shapes=[pltpu.VMEM((rows, width), jnp.float32)],
        compiler_params=pltpu.CompilerParams(
            dimension_semantics=("arbitrary",), vmem_limit_bytes=48 * 1024 * 1024
        ),
        cost_estimate=pl.CostEstimate(
            flops=2 * slots * tokens * rows * width,
            transcendentals=0,
            bytes_accessed=2 * slots * tokens * (rows + width) + 2 * rows * width,
        ),
    )(cols, *ctx_parts)


def on_device(queries, key_heads, value_heads, context_grad, output_grad, random_blocks):
    dp_count = lax.axis_size("dp")
    dp_pos = lax.axis_index("dp")
    pipe_count = lax.axis_size("pipe")
    pipe_pos = lax.axis_index("pipe")
    upper_half = (pipe_pos >= pipe_count // 2).astype(jnp.int32)
    rows_here = output_grad.shape[2]
    width_model = output_grad.shape[3]
    quarter = width_model // (2 * dp_count)
    pieces = output_grad[0, 0].reshape(rows_here, 2, dp_count, quarter).transpose(2, 1, 0, 3)
    received = [lax.dynamic_index_in_dim(pieces, dp_pos, 0, keepdims=False)]
    for shift in range(1, dp_count):
        target = (dp_pos + shift) % dp_count
        outgoing = lax.dynamic_index_in_dim(pieces, target, 0, keepdims=False)
        received.append(shift_over(outgoing, "dp", shift))
    moved = jnp.stack(received)
    send_cols = lax.dynamic_index_in_dim(moved, 1 - upper_half, 1, keepdims=False)
    keep_cols = lax.dynamic_index_in_dim(moved, upper_half, 1, keepdims=False)
    send_all = lax.all_gather(send_cols, "tensor", axis=1, tiled=True)
    keep_all = lax.all_gather(keep_cols, "tensor", axis=1, tiled=True)

    query_grad, key_grad, value_grad, ctx_rows = attention_backward(
        queries[0, 0], key_heads[0, 0], value_heads[0, 0], context_grad[0, 0], random_blocks
    )
    tokens_all = ctx_rows.shape[0]
    split = tokens_all // 2
    from_left = shift_over(ctx_rows, "dp", 1)
    from_right = shift_over(ctx_rows, "dp", -1)
    far_lo = shift_over(from_left[:split], "dp", 1)
    far_hi = shift_over(from_right[split:], "dp", -1)
    ctx_parts = (ctx_rows, from_left, far_lo, far_hi, from_right)

    send_block = weight_block(send_all, ctx_parts)
    incoming = lax.ppermute(
        send_block, "pipe", [(i, pipe_count - 1 - i) for i in range(pipe_count)]
    )
    keep_block = weight_block(keep_all, ctx_parts)
    weight_grad = (keep_block.astype(jnp.float32) + incoming.astype(jnp.float32)).astype(
        jnp.bfloat16
    )[None]
    shape4 = queries.shape
    return (
        query_grad.reshape(shape4),
        key_grad.reshape(shape4),
        value_grad.reshape(shape4),
        weight_grad,
    )


def solution(mesh):
    in_specs = (
        P("pipe", "dp", None, "tensor"),
        P("pipe", "dp", None, "tensor"),
        P("pipe", "dp", None, "tensor"),
        P("pipe", "dp", None, "tensor"),
        P("pipe", "dp", "tensor", None),
        P("tensor", None, None),
    )
    out_specs = (
        P("pipe", "dp", None, "tensor"),
        P("pipe", "dp", None, "tensor"),
        P("pipe", "dp", None, "tensor"),
        P("pipe", "dp", "tensor"),
    )
    return jax.shard_map(
        on_device, mesh=mesh, in_specs=in_specs, out_specs=out_specs, check_vma=False
    )
```

```python
import functools
import math

import jax
import jax.numpy as jnp
from jax import lax
from jax.experimental import pallas as pl
from jax.experimental.pallas import tpu as pltpu
from jax.sharding import PartitionSpec as P

BLK = 64
ROWS = 256


def attention_kernel(
    blocks, head_size, rb_ref, q_ref, k_ref, v_ref, g_ref, dq_ref, ctx_ref, dk_ref, dv_ref,
    dk_acc, dv_acc,
):
    head = pl.program_id(0)
    chunk = pl.program_id(1)
    score_scale = 1.0 / math.sqrt(head_size)
    tokens = k_ref.shape[0]
    per_chunk = q_ref.shape[0] // BLK
    mids = blocks - 2

    @pl.when(chunk == 0)
    def _():
        dk_acc[...] = jnp.zeros_like(dk_acc)
        dv_acc[...] = jnp.zeros_like(dv_acc)

    q = q_ref[...]
    k = k_ref[...]
    v = v_ref[...]
    g = g_ref[...]
    scores = lax.dot_general(
        q, k, (((1,), (1,)), ((), ())), preferred_element_type=jnp.float32
    ) * score_scale
    key_block = lax.broadcasted_iota(jnp.int32, (1, tokens), 1) // BLK
    bias_rows = []
    for i in range(per_chunk):
        qb = chunk * per_chunk + i
        row = jnp.clip(qb - 1, 0, mids - 1)
        base = (head * mids + row) * 3
        r1 = rb_ref[base]
        r2 = rb_ref[base + 1]
        r3 = rb_ref[base + 2]
        edge = jnp.logical_or(qb == 0, qb == blocks - 1)
        near = jnp.abs(key_block - qb) <= 1
        allowed = (
            (key_block == 0)
            | (key_block == blocks - 1)
            | near
            | (key_block == r1)
            | (key_block == r2)
            | (key_block == r3)
            | edge
        )
        bias = jnp.where(allowed, 0.0, -1e30).astype(jnp.float32)
        bias_rows.append(jnp.broadcast_to(bias, (BLK, tokens)))
    scores = scores + jnp.concatenate(bias_rows, axis=0)
    row_peak = jnp.max(scores, axis=1, keepdims=True)
    raised = jnp.exp(scores - row_peak)
    prob = raised / jnp.sum(raised, axis=1, keepdims=True)
    prob_b = prob.astype(jnp.bfloat16)
    ctx = jnp.dot(prob_b, v, preferred_element_type=jnp.float32).astype(jnp.bfloat16)
    ctx_ref[...] = ctx
    dprob = lax.dot_general(
        g, v, (((1,), (1,)), ((), ())), preferred_element_type=jnp.float32
    )
    row_dot = jnp.sum(
        g.astype(jnp.float32) * ctx.astype(jnp.float32), axis=1, keepdims=True
    )
    dscore = (prob * (dprob - row_dot)).astype(jnp.bfloat16)
    dq = jnp.dot(dscore, k, preferred_element_type=jnp.float32) * score_scale
    dq_ref[...] = dq.astype(jnp.bfloat16)
    dk_acc[...] += lax.dot_general(
        dscore, q, (((0,), (0,)), ((), ())), preferred_element_type=jnp.float32
    )
    dv_acc[...] += lax.dot_general(
        prob_b, g, (((0,), (0,)), ((), ())), preferred_element_type=jnp.float32
    )

    @pl.when(chunk == pl.num_programs(1) - 1)
    def _():
        dk_ref[...] = (dk_acc[...] * score_scale).astype(jnp.bfloat16)
        dv_ref[...] = dv_acc[...].astype(jnp.bfloat16)


def attention_backward(queries, key_heads, value_heads, context_grad, random_blocks):
    heads_here = random_blocks.shape[0]
    tokens, width_here = queries.shape
    head_size = width_here // heads_here
    blocks = tokens // BLK
    chunks = tokens // ROWS
    rb_flat = random_blocks.reshape(-1)
    row_spec = pl.BlockSpec((ROWS, head_size), lambda h, c, rb: (c, h))
    full_spec = pl.BlockSpec((tokens, head_size), lambda h, c, rb: (0, h))
    out_shape = jax.ShapeDtypeStruct((tokens, width_here), jnp.bfloat16)
    flops = 2 * tokens * tokens * head_size * 6 * heads_here
    call = pl.pallas_call(
        functools.partial(attention_kernel, blocks, head_size),
        out_shape=(out_shape, out_shape, out_shape, out_shape),
        grid_spec=pltpu.PrefetchScalarGridSpec(
            num_scalar_prefetch=1,
            grid=(heads_here, chunks),
            in_specs=[row_spec, full_spec, full_spec, row_spec],
            out_specs=[row_spec, row_spec, full_spec, full_spec],
            scratch_shapes=[
                pltpu.VMEM((tokens, head_size), jnp.float32),
                pltpu.VMEM((tokens, head_size), jnp.float32),
            ],
        ),
        compiler_params=pltpu.CompilerParams(
            dimension_semantics=("arbitrary", "arbitrary"),
            vmem_limit_bytes=48 * 1024 * 1024,
        ),
        cost_estimate=pl.CostEstimate(
            flops=flops,
            transcendentals=tokens * tokens * heads_here,
            bytes_accessed=7 * tokens * width_here * 2,
        ),
    )
    query_grad, context, key_grad, value_grad = call(
        rb_flat, queries, key_heads, value_heads, context_grad
    )
    return query_grad, key_grad, value_grad, context


def shift_over(block, axis, shift):
    count = lax.axis_size(axis)
    return lax.ppermute(block, axis, [(i, (i + shift) % count) for i in range(count)])


def wgrad_kernel(
    cols0_ref, cols_ref, own_ref, left_ref, far_lo_ref, far_hi_ref, right_ref, out_ref, acc
):
    slot = pl.program_id(0)
    half = far_lo_ref.shape[0]

    def term(cols, ctx):
        return lax.dot_general(
            cols, ctx, (((0,), (0,)), ((), ())), preferred_element_type=jnp.float32
        )

    @pl.when(slot == 0)
    def _():
        acc[...] = term(cols0_ref[...], own_ref[...])

    @pl.when(slot == 1)
    def _():
        acc[...] += term(cols_ref[...], left_ref[...])

    @pl.when(slot == 2)
    def _():
        acc[...] += term(cols_ref[:half, :], far_lo_ref[...]) + term(
            cols_ref[half:, :], far_hi_ref[...]
        )

    @pl.when(slot == 3)
    def _():
        out_ref[...] = (acc[...] + term(cols_ref[...], right_ref[...])).astype(out_ref.dtype)


def weight_block(cols0, cols, ctx_parts):
    others, tokens, rows = cols.shape
    width = ctx_parts[0].shape[1]
    full = pl.BlockSpec((tokens, width), lambda s: (0, 0))
    half = pl.BlockSpec((tokens // 2, width), lambda s: (0, 0))
    return pl.pallas_call(
        wgrad_kernel,
        out_shape=jax.ShapeDtypeStruct((rows, width), jnp.bfloat16),
        grid=(others + 1,),
        in_specs=[
            pl.BlockSpec((tokens, rows), lambda s: (0, 0)),
            pl.BlockSpec((None, tokens, rows), lambda s: (jnp.maximum(s - 1, 0), 0, 0)),
            full,
            full,
            half,
            half,
            full,
        ],
        out_specs=pl.BlockSpec((rows, width), lambda s: (0, 0)),
        scratch_shapes=[pltpu.VMEM((rows, width), jnp.float32)],
        compiler_params=pltpu.CompilerParams(
            dimension_semantics=("arbitrary",), vmem_limit_bytes=48 * 1024 * 1024
        ),
        cost_estimate=pl.CostEstimate(
            flops=2 * (others + 1) * tokens * rows * width,
            transcendentals=0,
            bytes_accessed=2 * (others + 1) * tokens * (rows + width) + 2 * rows * width,
        ),
    )(cols0, cols, *ctx_parts)


def gather_over_tensor(piece, tokens_all):
    count = lax.axis_size("tensor")
    pos = lax.axis_index("tensor")
    along_y = 4 if count % 4 == 0 else count
    along_z = count // along_y
    rows = piece.shape[1]
    out = jnp.zeros((piece.shape[0], tokens_all, piece.shape[2]), piece.dtype)
    out = lax.dynamic_update_slice(out, piece, (0, pos * rows, 0))
    zl = pos // along_y
    y = pos % along_y
    for dz in range(along_z):
        for dy in range(along_y):
            if dz == 0 and dy == 0:
                continue
            route = [
                (t, ((t // along_y + dz) % along_z) * along_y + (t % along_y + dy) % along_y)
                for t in range(count)
            ]
            got = lax.ppermute(piece, "tensor", route)
            src = ((zl - dz) % along_z) * along_y + (y - dy) % along_y
            out = lax.dynamic_update_slice(out, got, (0, src * rows, 0))
    return out


def on_device(queries, key_heads, value_heads, context_grad, output_grad, random_blocks):
    dp_count = lax.axis_size("dp")
    dp_pos = lax.axis_index("dp")
    pipe_count = lax.axis_size("pipe")
    pipe_pos = lax.axis_index("pipe")
    upper_half = (pipe_pos >= pipe_count // 2).astype(jnp.int32)
    rows_here = output_grad.shape[2]
    width_model = output_grad.shape[3]
    quarter = width_model // (2 * dp_count)
    pieces = output_grad[0, 0].reshape(rows_here, 2, dp_count, quarter).transpose(2, 1, 0, 3)
    pieces = jnp.where(upper_half == 1, pieces, pieces[:, ::-1])
    own_piece = lax.dynamic_index_in_dim(pieces, dp_pos, 0, keepdims=False)
    slot0 = gather_over_tensor(own_piece, output_grad.shape[2] * lax.axis_size("tensor"))
    received = []
    for shift in range(1, dp_count):
        target = (dp_pos + shift) % dp_count
        outgoing = lax.dynamic_index_in_dim(pieces, target, 0, keepdims=False)
        received.append(shift_over(outgoing, "dp", shift))
    moved = jnp.stack(received)
    send_all = lax.all_gather(moved[:, 0], "tensor", axis=1, tiled=True)
    keep_all = lax.all_gather(moved[:, 1], "tensor", axis=1, tiled=True)

    query_grad, key_grad, value_grad, ctx_rows = attention_backward(
        queries[0, 0], key_heads[0, 0], value_heads[0, 0], context_grad[0, 0], random_blocks
    )
    tokens_all = ctx_rows.shape[0]
    split = tokens_all // 2
    from_left = shift_over(ctx_rows, "dp", 1)
    from_right = shift_over(ctx_rows, "dp", -1)
    far_lo = shift_over(from_left[:split], "dp", 1)
    far_hi = shift_over(from_right[split:], "dp", -1)
    ctx_parts = (ctx_rows, from_left, far_lo, far_hi, from_right)

    send_block = weight_block(slot0[0], send_all, ctx_parts)
    incoming = lax.ppermute(
        send_block, "pipe", [(i, pipe_count - 1 - i) for i in range(pipe_count)]
    )
    keep_block = weight_block(slot0[1], keep_all, ctx_parts)
    weight_grad = (keep_block.astype(jnp.float32) + incoming.astype(jnp.float32)).astype(
        jnp.bfloat16
    )[None]
    shape4 = queries.shape
    return (
        query_grad.reshape(shape4),
        key_grad.reshape(shape4),
        value_grad.reshape(shape4),
        weight_grad,
    )


def solution(mesh):
    in_specs = (
        P("pipe", "dp", None, "tensor"),
        P("pipe", "dp", None, "tensor"),
        P("pipe", "dp", None, "tensor"),
        P("pipe", "dp", None, "tensor"),
        P("pipe", "dp", "tensor", None),
        P("tensor", None, None),
    )
    out_specs = (
        P("pipe", "dp", None, "tensor"),
        P("pipe", "dp", None, "tensor"),
        P("pipe", "dp", None, "tensor"),
        P("pipe", "dp", "tensor"),
    )
    return jax.shard_map(
        on_device, mesh=mesh, in_specs=in_specs, out_specs=out_specs, check_vma=False
    )
```

```python
import functools
import math

import jax
import jax.numpy as jnp
from jax import lax
from jax.experimental import pallas as pl
from jax.experimental.pallas import tpu as pltpu
from jax.sharding import PartitionSpec as P

BLK = 64
ROWS = 256


def attention_kernel(
    blocks, head_size, rb_ref, q_ref, k_ref, v_ref, g_ref, dq_ref, ctx_ref, dk_ref, dv_ref,
    dk_acc, dv_acc,
):
    head = pl.program_id(0)
    chunk = pl.program_id(1)
    score_scale = 1.0 / math.sqrt(head_size)
    tokens = k_ref.shape[0]
    per_chunk = q_ref.shape[0] // BLK
    mids = blocks - 2

    @pl.when(chunk == 0)
    def _():
        dk_acc[...] = jnp.zeros_like(dk_acc)
        dv_acc[...] = jnp.zeros_like(dv_acc)

    q = q_ref[...]
    k = k_ref[...]
    v = v_ref[...]
    g = g_ref[...]
    scores = lax.dot_general(
        q, k, (((1,), (1,)), ((), ())), preferred_element_type=jnp.float32
    ) * score_scale
    key_block = lax.broadcasted_iota(jnp.int32, (1, tokens), 1) // BLK
    bias_rows = []
    for i in range(per_chunk):
        qb = chunk * per_chunk + i
        row = jnp.clip(qb - 1, 0, mids - 1)
        base = (head * mids + row) * 3
        r1 = rb_ref[base]
        r2 = rb_ref[base + 1]
        r3 = rb_ref[base + 2]
        edge = jnp.logical_or(qb == 0, qb == blocks - 1)
        near = jnp.abs(key_block - qb) <= 1
        allowed = (
            (key_block == 0)
            | (key_block == blocks - 1)
            | near
            | (key_block == r1)
            | (key_block == r2)
            | (key_block == r3)
            | edge
        )
        bias = jnp.where(allowed, 0.0, -1e30).astype(jnp.float32)
        bias_rows.append(jnp.broadcast_to(bias, (BLK, tokens)))
    scores = scores + jnp.concatenate(bias_rows, axis=0)
    row_peak = jnp.max(scores, axis=1, keepdims=True)
    raised = jnp.exp(scores - row_peak)
    prob = raised / jnp.sum(raised, axis=1, keepdims=True)
    prob_b = prob.astype(jnp.bfloat16)
    ctx = jnp.dot(prob_b, v, preferred_element_type=jnp.float32).astype(jnp.bfloat16)
    ctx_ref[...] = ctx
    dprob = lax.dot_general(
        g, v, (((1,), (1,)), ((), ())), preferred_element_type=jnp.float32
    )
    row_dot = jnp.sum(
        g.astype(jnp.float32) * ctx.astype(jnp.float32), axis=1, keepdims=True
    )
    dscore = (prob * (dprob - row_dot)).astype(jnp.bfloat16)
    dq = jnp.dot(dscore, k, preferred_element_type=jnp.float32) * score_scale
    dq_ref[...] = dq.astype(jnp.bfloat16)
    dk_acc[...] += lax.dot_general(
        dscore, q, (((0,), (0,)), ((), ())), preferred_element_type=jnp.float32
    )
    dv_acc[...] += lax.dot_general(
        prob_b, g, (((0,), (0,)), ((), ())), preferred_element_type=jnp.float32
    )

    @pl.when(chunk == pl.num_programs(1) - 1)
    def _():
        dk_ref[...] = (dk_acc[...] * score_scale).astype(jnp.bfloat16)
        dv_ref[...] = dv_acc[...].astype(jnp.bfloat16)


def attention_backward(queries, key_heads, value_heads, context_grad, random_blocks):
    heads_here = random_blocks.shape[0]
    tokens, width_here = queries.shape
    head_size = width_here // heads_here
    blocks = tokens // BLK
    chunks = tokens // ROWS
    rb_flat = random_blocks.reshape(-1)
    row_spec = pl.BlockSpec((ROWS, head_size), lambda h, c, rb: (c, h))
    full_spec = pl.BlockSpec((tokens, head_size), lambda h, c, rb: (0, h))
    out_shape = jax.ShapeDtypeStruct((tokens, width_here), jnp.bfloat16)
    flops = 2 * tokens * tokens * head_size * 6 * heads_here
    call = pl.pallas_call(
        functools.partial(attention_kernel, blocks, head_size),
        out_shape=(out_shape, out_shape, out_shape, out_shape),
        grid_spec=pltpu.PrefetchScalarGridSpec(
            num_scalar_prefetch=1,
            grid=(heads_here, chunks),
            in_specs=[row_spec, full_spec, full_spec, row_spec],
            out_specs=[row_spec, row_spec, full_spec, full_spec],
            scratch_shapes=[
                pltpu.VMEM((tokens, head_size), jnp.float32),
                pltpu.VMEM((tokens, head_size), jnp.float32),
            ],
        ),
        compiler_params=pltpu.CompilerParams(
            dimension_semantics=("arbitrary", "arbitrary"),
            vmem_limit_bytes=48 * 1024 * 1024,
        ),
        cost_estimate=pl.CostEstimate(
            flops=flops,
            transcendentals=tokens * tokens * heads_here,
            bytes_accessed=7 * tokens * width_here * 2,
        ),
    )
    query_grad, context, key_grad, value_grad = call(
        rb_flat, queries, key_heads, value_heads, context_grad
    )
    return query_grad, key_grad, value_grad, context


def shift_over(block, axis, shift):
    count = lax.axis_size(axis)
    return lax.ppermute(block, axis, [(i, (i + shift) % count) for i in range(count)])


def wgrad_kernel(pieces, offs_ref, *refs):
    piece_refs = refs[:pieces]
    own_ref, left_ref, far_lo_ref, far_hi_ref, right_ref = refs[pieces : pieces + 5]
    out_ref, acc, buf = refs[pieces + 5 :]
    slot = pl.program_id(0)
    half = far_lo_ref.shape[0]
    for k, piece_ref in enumerate(piece_refs):
        start = pl.multiple_of(offs_ref[k], 64)
        buf[pl.ds(start, piece_ref.shape[0]), :] = piece_ref[...]

    def term(cols, ctx):
        return lax.dot_general(
            cols, ctx, (((0,), (0,)), ((), ())), preferred_element_type=jnp.float32
        )

    @pl.when(slot == 0)
    def _():
        acc[...] = term(buf[...], own_ref[...])

    @pl.when(slot == 1)
    def _():
        acc[...] += term(buf[...], left_ref[...])

    @pl.when(slot == 2)
    def _():
        acc[...] += term(buf[:half, :], far_lo_ref[...]) + term(buf[half:, :], far_hi_ref[...])

    @pl.when(slot == 3)
    def _():
        out_ref[...] = (acc[...] + term(buf[...], right_ref[...])).astype(out_ref.dtype)


def weight_block(piece_list, offsets, ctx_parts):
    slots = piece_list[0].shape[0]
    tokens, width = ctx_parts[0].shape
    rows = piece_list[0].shape[2]
    full = pl.BlockSpec((tokens, width), lambda s, o: (0, 0))
    half = pl.BlockSpec((tokens // 2, width), lambda s, o: (0, 0))
    piece_specs = [
        pl.BlockSpec((None, piece.shape[1], rows), lambda s, o: (s, 0, 0)) for piece in piece_list
    ]
    return pl.pallas_call(
        functools.partial(wgrad_kernel, len(piece_list)),
        out_shape=jax.ShapeDtypeStruct((rows, width), jnp.bfloat16),
        grid_spec=pltpu.PrefetchScalarGridSpec(
            num_scalar_prefetch=1,
            grid=(slots,),
            in_specs=piece_specs + [full, full, half, half, full],
            out_specs=pl.BlockSpec((rows, width), lambda s, o: (0, 0)),
            scratch_shapes=[
                pltpu.VMEM((rows, width), jnp.float32),
                pltpu.VMEM((tokens, rows), jnp.bfloat16),
            ],
        ),
        compiler_params=pltpu.CompilerParams(
            dimension_semantics=("arbitrary",), vmem_limit_bytes=48 * 1024 * 1024
        ),
        cost_estimate=pl.CostEstimate(
            flops=2 * slots * tokens * rows * width,
            transcendentals=0,
            bytes_accessed=2 * slots * tokens * (rows + width) + 2 * rows * width,
        ),
    )(offsets, *piece_list, *ctx_parts)


def gather_over_tensor(block):
    count = lax.axis_size("tensor")
    along_y = 4 if count % 4 == 0 else count
    along_z = count // along_y
    pos = lax.axis_index("tensor")
    zl = pos // along_y
    y = pos % along_y
    rows = block.shape[1]
    split = rows // 2

    def place(dz, dy):
        return (((zl + dz) % along_z) * along_y + (y + dy) % along_y) * rows

    def yshift(x, k):
        route = [(t, (t // along_y) * along_y + (t % along_y + k) % along_y) for t in range(count)]
        return lax.ppermute(x, "tensor", route)

    def zshift(x):
        route = [(t, ((t // along_y + 1) % along_z) * along_y + t % along_y) for t in range(count)]
        return lax.ppermute(x, "tensor", route)

    z_piece = zshift(block)
    from_left = yshift(block, 1)
    from_right = yshift(block, -1)
    z_left = yshift(z_piece, 1)
    z_right = yshift(z_piece, -1)
    far_a = yshift(from_left[:, :split], 1)
    far_b = yshift(from_right[:, split:], -1)
    z_far_a = zshift(far_a)
    z_far_b = zshift(far_b)
    pieces = [block, z_piece, from_left, from_right, z_left, z_right, far_a, far_b, z_far_a, z_far_b]
    offsets = [
        place(0, 0),
        place(1, 0),
        place(0, -1),
        place(0, 1),
        place(1, -1),
        place(1, 1),
        place(0, 2),
        place(0, 2) + split,
        place(1, 2),
        place(1, 2) + split,
    ]
    return pieces, jnp.stack(offsets).astype(jnp.int32)


def on_device(queries, key_heads, value_heads, context_grad, output_grad, random_blocks):
    dp_count = lax.axis_size("dp")
    dp_pos = lax.axis_index("dp")
    pipe_count = lax.axis_size("pipe")
    pipe_pos = lax.axis_index("pipe")
    upper_half = (pipe_pos >= pipe_count // 2).astype(jnp.int32)
    rows_here = output_grad.shape[2]
    width_model = output_grad.shape[3]
    quarter = width_model // (2 * dp_count)
    pieces = output_grad[0, 0].reshape(rows_here, 2, dp_count, quarter).transpose(2, 1, 0, 3)
    pieces = jnp.where(upper_half == 1, pieces, pieces[:, ::-1])
    received = [lax.dynamic_index_in_dim(pieces, dp_pos, 0, keepdims=False)]
    for shift in range(1, dp_count):
        target = (dp_pos + shift) % dp_count
        outgoing = lax.dynamic_index_in_dim(pieces, target, 0, keepdims=False)
        received.append(shift_over(outgoing, "dp", shift))
    moved = jnp.stack(received)
    send_pieces, offsets = gather_over_tensor(moved[:, 0])
    keep_pieces, _ = gather_over_tensor(moved[:, 1])

    query_grad, key_grad, value_grad, ctx_rows = attention_backward(
        queries[0, 0], key_heads[0, 0], value_heads[0, 0], context_grad[0, 0], random_blocks
    )
    tokens_all = ctx_rows.shape[0]
    split = tokens_all // 2
    from_left = shift_over(ctx_rows, "dp", 1)
    from_right = shift_over(ctx_rows, "dp", -1)
    far_lo = shift_over(from_left[:split], "dp", 1)
    far_hi = shift_over(from_right[split:], "dp", -1)
    ctx_parts = (ctx_rows, from_left, far_lo, far_hi, from_right)

    send_block = weight_block(send_pieces, offsets, ctx_parts)
    incoming = lax.ppermute(
        send_block, "pipe", [(i, pipe_count - 1 - i) for i in range(pipe_count)]
    )
    keep_block = weight_block(keep_pieces, offsets, ctx_parts)
    weight_grad = (keep_block.astype(jnp.float32) + incoming.astype(jnp.float32)).astype(
        jnp.bfloat16
    )[None]
    shape4 = queries.shape
    return (
        query_grad.reshape(shape4),
        key_grad.reshape(shape4),
        value_grad.reshape(shape4),
        weight_grad,
    )


def solution(mesh):
    in_specs = (
        P("pipe", "dp", None, "tensor"),
        P("pipe", "dp", None, "tensor"),
        P("pipe", "dp", None, "tensor"),
        P("pipe", "dp", None, "tensor"),
        P("pipe", "dp", "tensor", None),
        P("tensor", None, None),
    )
    out_specs = (
        P("pipe", "dp", None, "tensor"),
        P("pipe", "dp", None, "tensor"),
        P("pipe", "dp", None, "tensor"),
        P("pipe", "dp", "tensor"),
    )
    return jax.shard_map(
        on_device, mesh=mesh, in_specs=in_specs, out_specs=out_specs, check_vma=False
    )
```

```python
import functools
import math

import jax
import jax.numpy as jnp
from jax import lax
from jax.experimental import pallas as pl
from jax.experimental.pallas import tpu as pltpu
from jax.sharding import PartitionSpec as P

BLK = 64
ROWS = 256


def attention_kernel(blocks, head_size, head0, aliased, rb_ref, q_ref, k_ref, v_ref, g_ref, *rest):
    if aliased:
        rest = rest[4:]
    dq_ref, ctx_ref, dk_ref, dv_ref, dk_acc, dv_acc = rest
    head = pl.program_id(0) + head0
    chunk = pl.program_id(1)
    score_scale = 1.0 / math.sqrt(head_size)
    tokens = k_ref.shape[0]
    per_chunk = q_ref.shape[0] // BLK
    mids = blocks - 2

    @pl.when(chunk == 0)
    def _():
        dk_acc[...] = jnp.zeros_like(dk_acc)
        dv_acc[...] = jnp.zeros_like(dv_acc)

    q = q_ref[...]
    k = k_ref[...]
    v = v_ref[...]
    g = g_ref[...]
    scores = lax.dot_general(
        q, k, (((1,), (1,)), ((), ())), preferred_element_type=jnp.float32
    ) * score_scale
    key_block = lax.broadcasted_iota(jnp.int32, (1, tokens), 1) // BLK
    bias_rows = []
    for i in range(per_chunk):
        qb = chunk * per_chunk + i
        row = jnp.clip(qb - 1, 0, mids - 1)
        base = (head * mids + row) * 3
        r1 = rb_ref[base]
        r2 = rb_ref[base + 1]
        r3 = rb_ref[base + 2]
        edge = jnp.logical_or(qb == 0, qb == blocks - 1)
        near = jnp.abs(key_block - qb) <= 1
        allowed = (
            (key_block == 0)
            | (key_block == blocks - 1)
            | near
            | (key_block == r1)
            | (key_block == r2)
            | (key_block == r3)
            | edge
        )
        bias = jnp.where(allowed, 0.0, -1e30).astype(jnp.float32)
        bias_rows.append(jnp.broadcast_to(bias, (BLK, tokens)))
    scores = scores + jnp.concatenate(bias_rows, axis=0)
    row_peak = jnp.max(scores, axis=1, keepdims=True)
    raised = jnp.exp(scores - row_peak)
    prob = raised / jnp.sum(raised, axis=1, keepdims=True)
    prob_b = prob.astype(jnp.bfloat16)
    ctx = jnp.dot(prob_b, v, preferred_element_type=jnp.float32).astype(jnp.bfloat16)
    ctx_ref[...] = ctx
    dprob = lax.dot_general(
        g, v, (((1,), (1,)), ((), ())), preferred_element_type=jnp.float32
    )
    row_dot = jnp.sum(
        g.astype(jnp.float32) * ctx.astype(jnp.float32), axis=1, keepdims=True
    )
    dscore = (prob * (dprob - row_dot)).astype(jnp.bfloat16)
    dq = jnp.dot(dscore, k, preferred_element_type=jnp.float32) * score_scale
    dq_ref[...] = dq.astype(jnp.bfloat16)
    dk_acc[...] += lax.dot_general(
        dscore, q, (((0,), (0,)), ((), ())), preferred_element_type=jnp.float32
    )
    dv_acc[...] += lax.dot_general(
        prob_b, g, (((0,), (0,)), ((), ())), preferred_element_type=jnp.float32
    )

    @pl.when(chunk == pl.num_programs(1) - 1)
    def _():
        dk_ref[...] = (dk_acc[...] * score_scale).astype(jnp.bfloat16)
        dv_ref[...] = dv_acc[...].astype(jnp.bfloat16)


def attention_call(index, queries, key_heads, value_heads, context_grad, random_blocks, results):
    heads_here = random_blocks.shape[0]
    tokens, width_here = queries.shape
    head_size = width_here // heads_here
    blocks = tokens // BLK
    chunks = tokens // ROWS
    group = 2 if heads_here % 2 == 0 else 1
    head0 = index * group
    rb_flat = random_blocks.reshape(-1)
    out_shape = jax.ShapeDtypeStruct((tokens, width_here), jnp.bfloat16)
    row_spec = pl.BlockSpec((ROWS, head_size), lambda h, c, rb: (c, h + head0))
    full_spec = pl.BlockSpec((tokens, head_size), lambda h, c, rb: (0, h + head0))
    aliased = results is not None
    extra = [pl.BlockSpec(memory_space=pl.ANY)] * 4 if aliased else []
    call = pl.pallas_call(
        functools.partial(attention_kernel, blocks, head_size, head0, aliased),
        out_shape=(out_shape, out_shape, out_shape, out_shape),
        grid_spec=pltpu.PrefetchScalarGridSpec(
            num_scalar_prefetch=1,
            grid=(group, chunks),
            in_specs=[row_spec, full_spec, full_spec, row_spec] + extra,
            out_specs=[row_spec, row_spec, full_spec, full_spec],
            scratch_shapes=[
                pltpu.VMEM((tokens, head_size), jnp.float32),
                pltpu.VMEM((tokens, head_size), jnp.float32),
            ],
        ),
        input_output_aliases={5: 0, 6: 1, 7: 2, 8: 3} if aliased else {},
        compiler_params=pltpu.CompilerParams(
            dimension_semantics=("arbitrary", "arbitrary"),
            vmem_limit_bytes=48 * 1024 * 1024,
        ),
        cost_estimate=pl.CostEstimate(
            flops=2 * tokens * tokens * head_size * 6 * group,
            transcendentals=tokens * tokens * group,
            bytes_accessed=7 * tokens * head_size * group * 2,
        ),
    )
    args = (rb_flat, queries, key_heads, value_heads, context_grad)
    return call(*args, *results) if aliased else call(*args)


def shift_over(block, axis, shift):
    count = lax.axis_size(axis)
    return lax.ppermute(block, axis, [(i, (i + shift) % count) for i in range(count)])


def wgrad_kernel(pieces, offs_ref, *refs):
    piece_refs = refs[:pieces]
    own_ref, left_ref, far_lo_ref, far_hi_ref, right_ref = refs[pieces : pieces + 5]
    out_ref, acc, buf = refs[pieces + 5 :]
    slot = pl.program_id(0)
    half = far_lo_ref.shape[0]
    for k, piece_ref in enumerate(piece_refs):
        start = pl.multiple_of(offs_ref[k], 64)
        buf[pl.ds(start, piece_ref.shape[0]), :] = piece_ref[...]

    def term(cols, ctx):
        return lax.dot_general(
            cols, ctx, (((0,), (0,)), ((), ())), preferred_element_type=jnp.float32
        )

    @pl.when(slot == 0)
    def _():
        acc[...] = term(buf[...], own_ref[...])

    @pl.when(slot == 1)
    def _():
        acc[...] += term(buf[...], left_ref[...])

    @pl.when(slot == 2)
    def _():
        acc[...] += term(buf[:half, :], far_lo_ref[...]) + term(buf[half:, :], far_hi_ref[...])

    @pl.when(slot == 3)
    def _():
        out_ref[...] = (acc[...] + term(buf[...], right_ref[...])).astype(out_ref.dtype)


def weight_block(piece_list, offsets, ctx_parts):
    slots = piece_list[0].shape[0]
    tokens, width = ctx_parts[0].shape
    rows = piece_list[0].shape[2]
    full = pl.BlockSpec((tokens, width), lambda s, o: (0, 0))
    half = pl.BlockSpec((tokens // 2, width), lambda s, o: (0, 0))
    piece_specs = [
        pl.BlockSpec((None, piece.shape[1], rows), lambda s, o: (s, 0, 0)) for piece in piece_list
    ]
    return pl.pallas_call(
        functools.partial(wgrad_kernel, len(piece_list)),
        out_shape=jax.ShapeDtypeStruct((rows, width), jnp.bfloat16),
        grid_spec=pltpu.PrefetchScalarGridSpec(
            num_scalar_prefetch=1,
            grid=(slots,),
            in_specs=piece_specs + [full, full, half, half, full],
            out_specs=pl.BlockSpec((rows, width), lambda s, o: (0, 0)),
            scratch_shapes=[
                pltpu.VMEM((rows, width), jnp.float32),
                pltpu.VMEM((tokens, rows), jnp.bfloat16),
            ],
        ),
        compiler_params=pltpu.CompilerParams(
            dimension_semantics=("arbitrary",), vmem_limit_bytes=48 * 1024 * 1024
        ),
        cost_estimate=pl.CostEstimate(
            flops=2 * slots * tokens * rows * width,
            transcendentals=0,
            bytes_accessed=2 * slots * tokens * (rows + width) + 2 * rows * width,
        ),
    )(offsets, *piece_list, *ctx_parts)


def tensor_layout():
    count = lax.axis_size("tensor")
    along_y = 4 if count % 4 == 0 else count
    along_z = count // along_y
    return count, along_y, along_z


def yshift(x, k):
    count, along_y, _ = tensor_layout()
    route = [(t, (t // along_y) * along_y + (t % along_y + k) % along_y) for t in range(count)]
    return lax.ppermute(x, "tensor", route)


def zshift(x):
    count, along_y, along_z = tensor_layout()
    route = [(t, ((t // along_y + 1) % along_z) * along_y + t % along_y) for t in range(count)]
    return lax.ppermute(x, "tensor", route)


def gather_steps(block, last_over_z, between=lambda step, values: values):
    count, along_y, along_z = tensor_layout()
    pos = lax.axis_index("tensor")
    zl = pos // along_y
    y = pos % along_y
    rows = block.shape[1]
    split = rows // 2

    def place(dz, dy):
        return (((zl + dz) % along_z) * along_y + (y + dy) % along_y) * rows

    source = between(0, block)
    first = (zshift(source), yshift(source, 1), yshift(source, -1))
    z_piece, from_left, from_right = between(1, first)
    second = (
        yshift(z_piece, 1),
        yshift(z_piece, -1),
        yshift(from_left[:, :split], 1),
        yshift(from_right[:, split:], -1),
    )
    z_left, z_right, far_a, far_b = between(2, second)
    if last_over_z:
        third = (zshift(far_a), zshift(far_b))
    else:
        third = (yshift(z_left[:, :split], 1), yshift(z_right[:, split:], -1))
    pieces = [block, *first, *second, *third]
    offsets = [
        place(0, 0),
        place(1, 0),
        place(0, -1),
        place(0, 1),
        place(1, -1),
        place(1, 1),
        place(0, 2),
        place(0, 2) + split,
        place(1, 2),
        place(1, 2) + split,
    ]
    return pieces, jnp.stack(offsets).astype(jnp.int32)


def on_device(queries, key_heads, value_heads, context_grad, output_grad, random_blocks):
    dp_count = lax.axis_size("dp")
    dp_pos = lax.axis_index("dp")
    pipe_count = lax.axis_size("pipe")
    pipe_pos = lax.axis_index("pipe")
    upper_half = (pipe_pos >= pipe_count // 2).astype(jnp.int32)
    rows_here = output_grad.shape[2]
    width_model = output_grad.shape[3]
    quarter = width_model // (2 * dp_count)
    pieces = output_grad[0, 0].reshape(rows_here, 2, dp_count, quarter).transpose(2, 1, 0, 3)
    pieces = jnp.where(upper_half == 1, pieces, pieces[:, ::-1])
    received = [lax.dynamic_index_in_dim(pieces, dp_pos, 0, keepdims=False)]
    for shift in range(1, dp_count):
        target = (dp_pos + shift) % dp_count
        outgoing = lax.dynamic_index_in_dim(pieces, target, 0, keepdims=False)
        received.append(shift_over(outgoing, "dp", shift))
    moved = jnp.stack(received)
    attn_in = (queries[0, 0], key_heads[0, 0], value_heads[0, 0], context_grad[0, 0])
    calls = 3 if random_blocks.shape[0] % 6 == 0 else random_blocks.shape[0]
    state = {"results": None}

    def between(step, values):
        if step < calls:
            state["results"] = attention_call(
                step, *attn_in, random_blocks, state["results"]
            )
        values, _ = lax.optimization_barrier((values, state["results"][1]))
        return values

    send_pieces, offsets = gather_steps(moved[:, 0], True, between)
    for index in range(3, calls):
        state["results"] = attention_call(index, *attn_in, random_blocks, state["results"])
    keep_pieces, _ = gather_steps(moved[:, 1], False)
    query_grad, ctx_rows, key_grad, value_grad = state["results"]
    tokens_all = ctx_rows.shape[0]
    split = tokens_all // 2
    from_left = shift_over(ctx_rows, "dp", 1)
    from_right = shift_over(ctx_rows, "dp", -1)
    far_lo = shift_over(from_left[:split], "dp", 1)
    far_hi = shift_over(from_right[split:], "dp", -1)
    ctx_parts = (ctx_rows, from_left, far_lo, far_hi, from_right)

    send_block = weight_block(send_pieces, offsets, ctx_parts)
    incoming = lax.ppermute(
        send_block, "pipe", [(i, pipe_count - 1 - i) for i in range(pipe_count)]
    )
    keep_block = weight_block(keep_pieces, offsets, ctx_parts)
    weight_grad = (keep_block.astype(jnp.float32) + incoming.astype(jnp.float32)).astype(
        jnp.bfloat16
    )[None]
    shape4 = queries.shape
    return (
        query_grad.reshape(shape4),
        key_grad.reshape(shape4),
        value_grad.reshape(shape4),
        weight_grad,
    )


def solution(mesh):
    in_specs = (
        P("pipe", "dp", None, "tensor"),
        P("pipe", "dp", None, "tensor"),
        P("pipe", "dp", None, "tensor"),
        P("pipe", "dp", None, "tensor"),
        P("pipe", "dp", "tensor", None),
        P("tensor", None, None),
    )
    out_specs = (
        P("pipe", "dp", None, "tensor"),
        P("pipe", "dp", None, "tensor"),
        P("pipe", "dp", None, "tensor"),
        P("pipe", "dp", "tensor"),
    )
    return jax.shard_map(
        on_device, mesh=mesh, in_specs=in_specs, out_specs=out_specs, check_vma=False
    )
```

```python
import functools
import math

import jax
import jax.numpy as jnp
from jax import lax
from jax.experimental import pallas as pl
from jax.experimental.pallas import tpu as pltpu
from jax.sharding import PartitionSpec as P

BLK = 64
ROWS = 256


def attention_kernel(blocks, head_size, head0, aliased, rb_ref, q_ref, k_ref, v_ref, g_ref, *rest):
    if aliased:
        rest = rest[4:]
    dq_ref, ctx_ref, dk_ref, dv_ref, dk_acc, dv_acc = rest
    head = pl.program_id(0) + head0
    chunk = pl.program_id(1)
    score_scale = 1.0 / math.sqrt(head_size)
    tokens = k_ref.shape[0]
    per_chunk = q_ref.shape[0] // BLK
    mids = blocks - 2

    @pl.when(chunk == 0)
    def _():
        dk_acc[...] = jnp.zeros_like(dk_acc)
        dv_acc[...] = jnp.zeros_like(dv_acc)

    q = q_ref[...]
    k = k_ref[...]
    v = v_ref[...]
    g = g_ref[...]
    scores = lax.dot_general(
        q, k, (((1,), (1,)), ((), ())), preferred_element_type=jnp.float32
    ) * score_scale
    key_block = lax.broadcasted_iota(jnp.int32, (1, tokens), 1) // BLK
    bias_rows = []
    for i in range(per_chunk):
        qb = chunk * per_chunk + i
        row = jnp.clip(qb - 1, 0, mids - 1)
        base = (head * mids + row) * 3
        r1 = rb_ref[base]
        r2 = rb_ref[base + 1]
        r3 = rb_ref[base + 2]
        edge = jnp.logical_or(qb == 0, qb == blocks - 1)
        near = jnp.abs(key_block - qb) <= 1
        allowed = (
            (key_block == 0)
            | (key_block == blocks - 1)
            | near
            | (key_block == r1)
            | (key_block == r2)
            | (key_block == r3)
            | edge
        )
        bias = jnp.where(allowed, 0.0, -1e30).astype(jnp.float32)
        bias_rows.append(jnp.broadcast_to(bias, (BLK, tokens)))
    scores = scores + jnp.concatenate(bias_rows, axis=0)
    row_peak = jnp.max(scores, axis=1, keepdims=True)
    raised = jnp.exp(scores - row_peak)
    prob = raised / jnp.sum(raised, axis=1, keepdims=True)
    prob_b = prob.astype(jnp.bfloat16)
    ctx = jnp.dot(prob_b, v, preferred_element_type=jnp.float32).astype(jnp.bfloat16)
    ctx_ref[...] = ctx
    dprob = lax.dot_general(
        g, v, (((1,), (1,)), ((), ())), preferred_element_type=jnp.float32
    )
    row_dot = jnp.sum(
        g.astype(jnp.float32) * ctx.astype(jnp.float32), axis=1, keepdims=True
    )
    dscore = (prob * (dprob - row_dot)).astype(jnp.bfloat16)
    dq = jnp.dot(dscore, k, preferred_element_type=jnp.float32) * score_scale
    dq_ref[...] = dq.astype(jnp.bfloat16)
    dk_acc[...] += lax.dot_general(
        dscore, q, (((0,), (0,)), ((), ())), preferred_element_type=jnp.float32
    )
    dv_acc[...] += lax.dot_general(
        prob_b, g, (((0,), (0,)), ((), ())), preferred_element_type=jnp.float32
    )

    @pl.when(chunk == pl.num_programs(1) - 1)
    def _():
        dk_ref[...] = (dk_acc[...] * score_scale).astype(jnp.bfloat16)
        dv_ref[...] = dv_acc[...].astype(jnp.bfloat16)


def attention_call(index, queries, key_heads, value_heads, context_grad, random_blocks, results):
    heads_here = random_blocks.shape[0]
    tokens, width_here = queries.shape
    head_size = width_here // heads_here
    blocks = tokens // BLK
    chunks = tokens // ROWS
    group = 2 if heads_here % 2 == 0 else 1
    head0 = index * group
    rb_flat = random_blocks.reshape(-1)
    out_shape = jax.ShapeDtypeStruct((tokens, width_here), jnp.bfloat16)
    row_spec = pl.BlockSpec((ROWS, head_size), lambda h, c, rb: (c, h + head0))
    full_spec = pl.BlockSpec((tokens, head_size), lambda h, c, rb: (0, h + head0))
    aliased = results is not None
    extra = [pl.BlockSpec(memory_space=pl.ANY)] * 4 if aliased else []
    call = pl.pallas_call(
        functools.partial(attention_kernel, blocks, head_size, head0, aliased),
        out_shape=(out_shape, out_shape, out_shape, out_shape),
        grid_spec=pltpu.PrefetchScalarGridSpec(
            num_scalar_prefetch=1,
            grid=(group, chunks),
            in_specs=[row_spec, full_spec, full_spec, row_spec] + extra,
            out_specs=[row_spec, row_spec, full_spec, full_spec],
            scratch_shapes=[
                pltpu.VMEM((tokens, head_size), jnp.float32),
                pltpu.VMEM((tokens, head_size), jnp.float32),
            ],
        ),
        input_output_aliases={5: 0, 6: 1, 7: 2, 8: 3} if aliased else {},
        compiler_params=pltpu.CompilerParams(
            dimension_semantics=("arbitrary", "arbitrary"),
            vmem_limit_bytes=48 * 1024 * 1024,
        ),
        cost_estimate=pl.CostEstimate(
            flops=2 * tokens * tokens * head_size * 6 * group,
            transcendentals=tokens * tokens * group,
            bytes_accessed=7 * tokens * head_size * group * 2,
        ),
    )
    args = (rb_flat, queries, key_heads, value_heads, context_grad)
    return call(*args, *results) if aliased else call(*args)


def shift_over(block, axis, shift):
    count = lax.axis_size(axis)
    return lax.ppermute(block, axis, [(i, (i + shift) % count) for i in range(count)])


def wgrad_kernel(pieces, widths, offs_ref, *refs):
    groups = len(widths)
    piece_refs = refs[:pieces]
    ctx_refs = refs[pieces : pieces + 5 * groups]
    out_ref, acc, buf = refs[pieces + 5 * groups :]
    slot = pl.program_id(0)
    for k, piece_ref in enumerate(piece_refs):
        start = pl.multiple_of(offs_ref[k], 64)
        buf[pl.ds(start, piece_ref.shape[0]), :] = piece_ref[...]

    def term(cols, ctx):
        return lax.dot_general(
            cols, ctx, (((0,), (0,)), ((), ())), preferred_element_type=jnp.float32
        )

    col0 = 0
    for g, width in enumerate(widths):
        own_ref, left_ref, far_lo_ref, far_hi_ref, right_ref = ctx_refs[5 * g : 5 * g + 5]
        half = far_lo_ref.shape[0]
        cols = slice(col0, col0 + width)

        @pl.when(slot == 0)
        def _():
            acc[:, cols] = term(buf[...], own_ref[...])

        @pl.when(slot == 1)
        def _():
            acc[:, cols] += term(buf[...], left_ref[...])

        @pl.when(slot == 2)
        def _():
            acc[:, cols] += term(buf[:half, :], far_lo_ref[...]) + term(
                buf[half:, :], far_hi_ref[...]
            )

        @pl.when(slot == 3)
        def _():
            out_ref[:, cols] = (acc[:, cols] + term(buf[...], right_ref[...])).astype(
                out_ref.dtype
            )

        col0 += width


def weight_block(piece_list, offsets, ctx_groups):
    slots = piece_list[0].shape[0]
    tokens = ctx_groups[0][0].shape[0]
    widths = tuple(group[0].shape[1] for group in ctx_groups)
    width = sum(widths)
    rows = piece_list[0].shape[2]
    piece_specs = [
        pl.BlockSpec((None, piece.shape[1], rows), lambda s, o: (s, 0, 0)) for piece in piece_list
    ]
    ctx_specs = []
    for group in ctx_groups:
        ctx_specs += [pl.BlockSpec(part.shape, lambda s, o: (0, 0)) for part in group]
    ctx_flat = [part for group in ctx_groups for part in group]
    return pl.pallas_call(
        functools.partial(wgrad_kernel, len(piece_list), widths),
        out_shape=jax.ShapeDtypeStruct((rows, width), jnp.bfloat16),
        grid_spec=pltpu.PrefetchScalarGridSpec(
            num_scalar_prefetch=1,
            grid=(slots,),
            in_specs=piece_specs + ctx_specs,
            out_specs=pl.BlockSpec((rows, width), lambda s, o: (0, 0)),
            scratch_shapes=[
                pltpu.VMEM((rows, width), jnp.float32),
                pltpu.VMEM((tokens, rows), jnp.bfloat16),
            ],
        ),
        compiler_params=pltpu.CompilerParams(
            dimension_semantics=("arbitrary",), vmem_limit_bytes=48 * 1024 * 1024
        ),
        cost_estimate=pl.CostEstimate(
            flops=2 * slots * tokens * rows * width,
            transcendentals=0,
            bytes_accessed=2 * slots * tokens * (rows + width) + 2 * rows * width,
        ),
    )(offsets, *piece_list, *ctx_flat)


def ring_over_dp(ctx_rows):
    split = ctx_rows.shape[0] // 2
    from_left = shift_over(ctx_rows, "dp", 1)
    from_right = shift_over(ctx_rows, "dp", -1)
    far_lo = shift_over(from_left[:split], "dp", 1)
    far_hi = shift_over(from_right[split:], "dp", -1)
    return (ctx_rows, from_left, far_lo, far_hi, from_right)


def tensor_layout():
    count = lax.axis_size("tensor")
    along_y = 4 if count % 4 == 0 else count
    along_z = count // along_y
    return count, along_y, along_z


def yshift(x, k):
    count, along_y, _ = tensor_layout()
    route = [(t, (t // along_y) * along_y + (t % along_y + k) % along_y) for t in range(count)]
    return lax.ppermute(x, "tensor", route)


def zshift(x):
    count, along_y, along_z = tensor_layout()
    route = [(t, ((t // along_y + 1) % along_z) * along_y + t % along_y) for t in range(count)]
    return lax.ppermute(x, "tensor", route)


def gather_steps(block, last_over_z, between=lambda step, values: values):
    count, along_y, along_z = tensor_layout()
    pos = lax.axis_index("tensor")
    zl = pos // along_y
    y = pos % along_y
    rows = block.shape[1]
    split = rows // 2

    def place(dz, dy):
        return (((zl + dz) % along_z) * along_y + (y + dy) % along_y) * rows

    source = between(0, block)
    first = (zshift(source), yshift(source, 1), yshift(source, -1))
    z_piece, from_left, from_right = between(1, first)
    second = (
        yshift(z_piece, 1),
        yshift(z_piece, -1),
        yshift(from_left[:, :split], 1),
        yshift(from_right[:, split:], -1),
    )
    z_left, z_right, far_a, far_b = between(2, second)
    if last_over_z:
        third = (zshift(far_a), zshift(far_b))
    else:
        third = (yshift(z_left[:, :split], 1), yshift(z_right[:, split:], -1))
    pieces = [block, *first, *second, *third]
    offsets = [
        place(0, 0),
        place(1, 0),
        place(0, -1),
        place(0, 1),
        place(1, -1),
        place(1, 1),
        place(0, 2),
        place(0, 2) + split,
        place(1, 2),
        place(1, 2) + split,
    ]
    return pieces, jnp.stack(offsets).astype(jnp.int32)


def on_device(queries, key_heads, value_heads, context_grad, output_grad, random_blocks):
    dp_count = lax.axis_size("dp")
    dp_pos = lax.axis_index("dp")
    pipe_count = lax.axis_size("pipe")
    pipe_pos = lax.axis_index("pipe")
    upper_half = (pipe_pos >= pipe_count // 2).astype(jnp.int32)
    rows_here = output_grad.shape[2]
    width_model = output_grad.shape[3]
    quarter = width_model // (2 * dp_count)
    pieces = output_grad[0, 0].reshape(rows_here, 2, dp_count, quarter).transpose(2, 1, 0, 3)
    pieces = jnp.where(upper_half == 1, pieces, pieces[:, ::-1])
    received = [lax.dynamic_index_in_dim(pieces, dp_pos, 0, keepdims=False)]
    for shift in range(1, dp_count):
        target = (dp_pos + shift) % dp_count
        outgoing = lax.dynamic_index_in_dim(pieces, target, 0, keepdims=False)
        received.append(shift_over(outgoing, "dp", shift))
    moved = jnp.stack(received)
    attn_in = (queries[0, 0], key_heads[0, 0], value_heads[0, 0], context_grad[0, 0])
    calls = 3 if random_blocks.shape[0] % 6 == 0 else random_blocks.shape[0]
    state = {"results": None, "after": []}

    def between(step, values):
        if step < calls:
            state["results"] = attention_call(
                step, *attn_in, random_blocks, state["results"]
            )
            state["after"].append(state["results"])
        values, _ = lax.optimization_barrier((values, state["results"][1]))
        return values

    send_pieces, offsets = gather_steps(moved[:, 0], True, between)
    for index in range(3, calls):
        state["results"] = attention_call(index, *attn_in, random_blocks, state["results"])
    keep_pieces, _ = gather_steps(moved[:, 1], False)
    query_grad, ctx_rows, key_grad, value_grad = state["results"]
    early = state["after"][-2][1] if len(state["after"]) >= 2 else None
    if early is not None and ctx_rows.shape[1] % 3 == 0:
        cut = ctx_rows.shape[1] * 2 // 3
        ctx_groups = (ring_over_dp(early[:, :cut]), ring_over_dp(ctx_rows[:, cut:]))
    else:
        ctx_groups = (ring_over_dp(ctx_rows),)

    send_block = weight_block(send_pieces, offsets, ctx_groups)
    incoming = lax.ppermute(
        send_block, "pipe", [(i, pipe_count - 1 - i) for i in range(pipe_count)]
    )
    keep_block = weight_block(keep_pieces, offsets, ctx_groups)
    weight_grad = (keep_block.astype(jnp.float32) + incoming.astype(jnp.float32)).astype(
        jnp.bfloat16
    )[None]
    shape4 = queries.shape
    return (
        query_grad.reshape(shape4),
        key_grad.reshape(shape4),
        value_grad.reshape(shape4),
        weight_grad,
    )


def solution(mesh):
    in_specs = (
        P("pipe", "dp", None, "tensor"),
        P("pipe", "dp", None, "tensor"),
        P("pipe", "dp", None, "tensor"),
        P("pipe", "dp", None, "tensor"),
        P("pipe", "dp", "tensor", None),
        P("tensor", None, None),
    )
    out_specs = (
        P("pipe", "dp", None, "tensor"),
        P("pipe", "dp", None, "tensor"),
        P("pipe", "dp", None, "tensor"),
        P("pipe", "dp", "tensor"),
    )
    return jax.shard_map(
        on_device, mesh=mesh, in_specs=in_specs, out_specs=out_specs, check_vma=False
    )
```

```python
import functools
import math

import jax
import jax.numpy as jnp
from jax import lax
from jax.experimental import pallas as pl
from jax.experimental.pallas import tpu as pltpu
from jax.sharding import PartitionSpec as P

BLK = 64
ROWS = 256


def attention_kernel(blocks, head_size, head0, aliased, rb_ref, q_ref, k_ref, v_ref, g_ref, *rest):
    if aliased:
        rest = rest[4:]
    dq_ref, ctx_ref, dk_ref, dv_ref, dk_acc, dv_acc = rest
    head = pl.program_id(0) + head0
    chunk = pl.program_id(1)
    score_scale = 1.0 / math.sqrt(head_size)
    tokens = k_ref.shape[0]
    per_chunk = q_ref.shape[0] // BLK
    mids = blocks - 2

    @pl.when(chunk == 0)
    def _():
        dk_acc[...] = jnp.zeros_like(dk_acc)
        dv_acc[...] = jnp.zeros_like(dv_acc)

    q = q_ref[...]
    k = k_ref[...]
    v = v_ref[...]
    g = g_ref[...]
    scores = lax.dot_general(
        q, k, (((1,), (1,)), ((), ())), preferred_element_type=jnp.float32
    ) * score_scale
    key_block = lax.broadcasted_iota(jnp.int32, (1, tokens), 1) // BLK
    bias_rows = []
    for i in range(per_chunk):
        qb = chunk * per_chunk + i
        row = jnp.clip(qb - 1, 0, mids - 1)
        base = (head * mids + row) * 3
        r1 = rb_ref[base]
        r2 = rb_ref[base + 1]
        r3 = rb_ref[base + 2]
        edge = jnp.logical_or(qb == 0, qb == blocks - 1)
        near = jnp.abs(key_block - qb) <= 1
        allowed = (
            (key_block == 0)
            | (key_block == blocks - 1)
            | near
            | (key_block == r1)
            | (key_block == r2)
            | (key_block == r3)
            | edge
        )
        bias = jnp.where(allowed, 0.0, -1e30).astype(jnp.float32)
        bias_rows.append(jnp.broadcast_to(bias, (BLK, tokens)))
    scores = scores + jnp.concatenate(bias_rows, axis=0)
    row_peak = jnp.max(scores, axis=1, keepdims=True)
    raised = jnp.exp(scores - row_peak)
    prob = raised / jnp.sum(raised, axis=1, keepdims=True)
    prob_b = prob.astype(jnp.bfloat16)
    ctx = jnp.dot(prob_b, v, preferred_element_type=jnp.float32).astype(jnp.bfloat16)
    ctx_ref[...] = ctx
    dprob = lax.dot_general(
        g, v, (((1,), (1,)), ((), ())), preferred_element_type=jnp.float32
    )
    row_dot = jnp.sum(
        g.astype(jnp.float32) * ctx.astype(jnp.float32), axis=1, keepdims=True
    )
    dscore = (prob * (dprob - row_dot)).astype(jnp.bfloat16)
    dq = jnp.dot(dscore, k, preferred_element_type=jnp.float32) * score_scale
    dq_ref[...] = dq.astype(jnp.bfloat16)
    dk_acc[...] += lax.dot_general(
        dscore, q, (((0,), (0,)), ((), ())), preferred_element_type=jnp.float32
    )
    dv_acc[...] += lax.dot_general(
        prob_b, g, (((0,), (0,)), ((), ())), preferred_element_type=jnp.float32
    )

    @pl.when(chunk == pl.num_programs(1) - 1)
    def _():
        dk_ref[...] = (dk_acc[...] * score_scale).astype(jnp.bfloat16)
        dv_ref[...] = dv_acc[...].astype(jnp.bfloat16)


def attention_call(index, queries, key_heads, value_heads, context_grad, random_blocks, results):
    heads_here = random_blocks.shape[0]
    tokens, width_here = queries.shape
    head_size = width_here // heads_here
    blocks = tokens // BLK
    chunks = tokens // ROWS
    group = 2 if heads_here % 2 == 0 else 1
    head0 = index * group
    rb_flat = random_blocks.reshape(-1)
    out_shape = jax.ShapeDtypeStruct((tokens, width_here), jnp.bfloat16)
    row_spec = pl.BlockSpec((ROWS, head_size), lambda h, c, rb: (c, h + head0))
    full_spec = pl.BlockSpec((tokens, head_size), lambda h, c, rb: (0, h + head0))
    aliased = results is not None
    extra = [pl.BlockSpec(memory_space=pl.ANY)] * 4 if aliased else []
    call = pl.pallas_call(
        functools.partial(attention_kernel, blocks, head_size, head0, aliased),
        out_shape=(out_shape, out_shape, out_shape, out_shape),
        grid_spec=pltpu.PrefetchScalarGridSpec(
            num_scalar_prefetch=1,
            grid=(group, chunks),
            in_specs=[row_spec, full_spec, full_spec, row_spec] + extra,
            out_specs=[row_spec, row_spec, full_spec, full_spec],
            scratch_shapes=[
                pltpu.VMEM((tokens, head_size), jnp.float32),
                pltpu.VMEM((tokens, head_size), jnp.float32),
            ],
        ),
        input_output_aliases={5: 0, 6: 1, 7: 2, 8: 3} if aliased else {},
        compiler_params=pltpu.CompilerParams(
            dimension_semantics=("arbitrary", "arbitrary"),
            vmem_limit_bytes=48 * 1024 * 1024,
        ),
        cost_estimate=pl.CostEstimate(
            flops=2 * tokens * tokens * head_size * 6 * group,
            transcendentals=tokens * tokens * group,
            bytes_accessed=7 * tokens * head_size * group * 2,
        ),
    )
    args = (rb_flat, queries, key_heads, value_heads, context_grad)
    return call(*args, *results) if aliased else call(*args)


def shift_over(block, axis, shift):
    count = lax.axis_size(axis)
    return lax.ppermute(block, axis, [(i, (i + shift) % count) for i in range(count)])


def wgrad_kernel(layout, widths, offs_ref, *refs):
    groups = len(widths)
    pieces = len(layout)
    piece_refs = refs[:pieces]
    ctx_refs = refs[pieces : pieces + 5 * groups]
    out_ref, acc, buf = refs[pieces + 5 * groups :]
    slot = pl.program_id(0)
    index = 0
    for piece_ref, parts in zip(piece_refs, layout):
        for first_row, count in parts:
            start = pl.multiple_of(offs_ref[index], 64)
            buf[pl.ds(start, count), :] = piece_ref[first_row : first_row + count, :]
            index += 1

    def term(cols, ctx):
        return lax.dot_general(
            cols, ctx, (((0,), (0,)), ((), ())), preferred_element_type=jnp.float32
        )

    col0 = 0
    for g, width in enumerate(widths):
        own_ref, left_ref, far_lo_ref, far_hi_ref, right_ref = ctx_refs[5 * g : 5 * g + 5]
        half = far_lo_ref.shape[0]
        cols = slice(col0, col0 + width)

        @pl.when(slot == 0)
        def _():
            acc[:, cols] = term(buf[...], own_ref[...])

        @pl.when(slot == 1)
        def _():
            acc[:, cols] += term(buf[...], left_ref[...])

        @pl.when(slot == 2)
        def _():
            acc[:, cols] += term(buf[:half, :], far_lo_ref[...]) + term(
                buf[half:, :], far_hi_ref[...]
            )

        @pl.when(slot == 3)
        def _():
            out_ref[:, cols] = (acc[:, cols] + term(buf[...], right_ref[...])).astype(
                out_ref.dtype
            )

        col0 += width


def weight_block(piece_list, layout, offsets, ctx_groups):
    slots = piece_list[0].shape[0]
    tokens = ctx_groups[0][0].shape[0]
    widths = tuple(group[0].shape[1] for group in ctx_groups)
    width = sum(widths)
    rows = piece_list[0].shape[2]
    piece_specs = [
        pl.BlockSpec((None, piece.shape[1], rows), lambda s, o: (s, 0, 0)) for piece in piece_list
    ]
    ctx_specs = []
    for group in ctx_groups:
        ctx_specs += [pl.BlockSpec(part.shape, lambda s, o: (0, 0)) for part in group]
    ctx_flat = [part for group in ctx_groups for part in group]
    return pl.pallas_call(
        functools.partial(wgrad_kernel, layout, widths),
        out_shape=jax.ShapeDtypeStruct((rows, width), jnp.bfloat16),
        grid_spec=pltpu.PrefetchScalarGridSpec(
            num_scalar_prefetch=1,
            grid=(slots,),
            in_specs=piece_specs + ctx_specs,
            out_specs=pl.BlockSpec((rows, width), lambda s, o: (0, 0)),
            scratch_shapes=[
                pltpu.VMEM((rows, width), jnp.float32),
                pltpu.VMEM((tokens, rows), jnp.bfloat16),
            ],
        ),
        compiler_params=pltpu.CompilerParams(
            dimension_semantics=("arbitrary",), vmem_limit_bytes=48 * 1024 * 1024
        ),
        cost_estimate=pl.CostEstimate(
            flops=2 * slots * tokens * rows * width,
            transcendentals=0,
            bytes_accessed=2 * slots * tokens * (rows + width) + 2 * rows * width,
        ),
    )(offsets, *piece_list, *ctx_flat)


def ring_over_dp(ctx_rows):
    split = ctx_rows.shape[0] // 2
    from_left = shift_over(ctx_rows, "dp", 1)
    from_right = shift_over(ctx_rows, "dp", -1)
    far_lo = shift_over(from_left[:split], "dp", 1)
    far_hi = shift_over(from_right[split:], "dp", -1)
    return (ctx_rows, from_left, far_lo, far_hi, from_right)


def tensor_layout():
    count = lax.axis_size("tensor")
    along_y = 4 if count % 4 == 0 else count
    along_z = count // along_y
    return count, along_y, along_z


def yshift(x, k):
    count, along_y, _ = tensor_layout()
    route = [(t, (t // along_y) * along_y + (t % along_y + k) % along_y) for t in range(count)]
    return lax.ppermute(x, "tensor", route)


def zshift(x):
    count, along_y, along_z = tensor_layout()
    route = [(t, ((t // along_y + 1) % along_z) * along_y + t % along_y) for t in range(count)]
    return lax.ppermute(x, "tensor", route)


def gather_steps(block, last_over_z, between=lambda step, values: values):
    count, along_y, along_z = tensor_layout()
    pos = lax.axis_index("tensor")
    zl = pos // along_y
    y = pos % along_y
    rows = block.shape[1]
    split = rows // 2

    def place(dz, dy):
        return (((zl + dz) % along_z) * along_y + (y + dy) % along_y) * rows

    source = between(0, block)
    first = (zshift(source), yshift(source, 1), yshift(source, -1))
    z_piece, from_left, from_right = between(1, first)
    second = (
        yshift(jnp.concatenate([z_piece, from_left[:, :split]], axis=1), 1),
        yshift(jnp.concatenate([z_piece, from_right[:, split:]], axis=1), -1),
    )
    plus, minus = between(2, second)
    if last_over_z:
        third = (zshift(plus[:, rows:]), zshift(minus[:, rows:]))
    else:
        third = (yshift(plus[:, :split], 1), yshift(minus[:, split:rows], -1))
    pieces = [block, *first, *second, *third]
    whole = ((0, rows),)
    layout = (whole,) * 4 + (((0, rows), (rows, split)),) * 2 + (((0, split),),) * 2
    offsets = [
        place(0, 0),
        place(1, 0),
        place(0, -1),
        place(0, 1),
        place(1, -1),
        place(0, 2),
        place(1, 1),
        place(0, 2) + split,
        place(1, 2),
        place(1, 2) + split,
    ]
    return pieces, layout, jnp.stack(offsets).astype(jnp.int32)


def on_device(queries, key_heads, value_heads, context_grad, output_grad, random_blocks):
    dp_count = lax.axis_size("dp")
    dp_pos = lax.axis_index("dp")
    pipe_count = lax.axis_size("pipe")
    pipe_pos = lax.axis_index("pipe")
    upper_half = (pipe_pos >= pipe_count // 2).astype(jnp.int32)
    rows_here = output_grad.shape[2]
    width_model = output_grad.shape[3]
    quarter = width_model // (2 * dp_count)
    pieces = output_grad[0, 0].reshape(rows_here, 2, dp_count, quarter).transpose(2, 1, 0, 3)
    pieces = jnp.where(upper_half == 1, pieces, pieces[:, ::-1])
    received = [lax.dynamic_index_in_dim(pieces, dp_pos, 0, keepdims=False)]
    for shift in range(1, dp_count):
        target = (dp_pos + shift) % dp_count
        outgoing = lax.dynamic_index_in_dim(pieces, target, 0, keepdims=False)
        received.append(shift_over(outgoing, "dp", shift))
    moved = jnp.stack(received)
    attn_in = (queries[0, 0], key_heads[0, 0], value_heads[0, 0], context_grad[0, 0])
    calls = 3 if random_blocks.shape[0] % 6 == 0 else random_blocks.shape[0]
    state = {"results": None, "after": []}

    def between(step, values):
        if step < calls:
            state["results"] = attention_call(
                step, *attn_in, random_blocks, state["results"]
            )
            state["after"].append(state["results"])
        values, _ = lax.optimization_barrier((values, state["results"][1]))
        return values

    send_pieces, send_layout, offsets = gather_steps(moved[:, 0], True, between)
    for index in range(3, calls):
        state["results"] = attention_call(index, *attn_in, random_blocks, state["results"])
    keep_pieces, keep_layout, _ = gather_steps(moved[:, 1], False)
    query_grad, ctx_rows, key_grad, value_grad = state["results"]
    early = state["after"][-2][1] if len(state["after"]) >= 2 else None
    if early is not None and ctx_rows.shape[1] % 3 == 0:
        cut = ctx_rows.shape[1] * 2 // 3
        ctx_groups = (ring_over_dp(early[:, :cut]), ring_over_dp(ctx_rows[:, cut:]))
    else:
        ctx_groups = (ring_over_dp(ctx_rows),)

    send_block = weight_block(send_pieces, send_layout, offsets, ctx_groups)
    incoming = lax.ppermute(
        send_block, "pipe", [(i, pipe_count - 1 - i) for i in range(pipe_count)]
    )
    keep_block = weight_block(keep_pieces, keep_layout, offsets, ctx_groups)
    weight_grad = (keep_block.astype(jnp.float32) + incoming.astype(jnp.float32)).astype(
        jnp.bfloat16
    )[None]
    shape4 = queries.shape
    return (
        query_grad.reshape(shape4),
        key_grad.reshape(shape4),
        value_grad.reshape(shape4),
        weight_grad,
    )


def solution(mesh):
    in_specs = (
        P("pipe", "dp", None, "tensor"),
        P("pipe", "dp", None, "tensor"),
        P("pipe", "dp", None, "tensor"),
        P("pipe", "dp", None, "tensor"),
        P("pipe", "dp", "tensor", None),
        P("tensor", None, None),
    )
    out_specs = (
        P("pipe", "dp", None, "tensor"),
        P("pipe", "dp", None, "tensor"),
        P("pipe", "dp", None, "tensor"),
        P("pipe", "dp", "tensor"),
    )
    return jax.shard_map(
        on_device, mesh=mesh, in_specs=in_specs, out_specs=out_specs, check_vma=False
    )
```

```python
import functools
import math

import jax
import jax.numpy as jnp
from jax import lax
from jax.experimental import pallas as pl
from jax.experimental.pallas import tpu as pltpu
from jax.sharding import PartitionSpec as P

BLK = 64
ROWS = 256


def attention_kernel(blocks, head_size, head0, aliased, rb_ref, q_ref, k_ref, v_ref, g_ref, *rest):
    if aliased:
        rest = rest[4:]
    dq_ref, ctx_ref, dk_ref, dv_ref, dk_acc, dv_acc = rest
    head = pl.program_id(0) + head0
    chunk = pl.program_id(1)
    score_scale = 1.0 / math.sqrt(head_size)
    tokens = k_ref.shape[0]
    per_chunk = q_ref.shape[0] // BLK
    mids = blocks - 2

    @pl.when(chunk == 0)
    def _():
        dk_acc[...] = jnp.zeros_like(dk_acc)
        dv_acc[...] = jnp.zeros_like(dv_acc)

    q = q_ref[...]
    k = k_ref[...]
    v = v_ref[...]
    g = g_ref[...]
    scores = lax.dot_general(
        q, k, (((1,), (1,)), ((), ())), preferred_element_type=jnp.float32
    ) * score_scale
    key_block = lax.broadcasted_iota(jnp.int32, (1, tokens), 1) // BLK
    bias_rows = []
    for i in range(per_chunk):
        qb = chunk * per_chunk + i
        row = jnp.clip(qb - 1, 0, mids - 1)
        base = (head * mids + row) * 3
        r1 = rb_ref[base]
        r2 = rb_ref[base + 1]
        r3 = rb_ref[base + 2]
        edge = jnp.logical_or(qb == 0, qb == blocks - 1)
        near = jnp.abs(key_block - qb) <= 1
        allowed = (
            (key_block == 0)
            | (key_block == blocks - 1)
            | near
            | (key_block == r1)
            | (key_block == r2)
            | (key_block == r3)
            | edge
        )
        bias = jnp.where(allowed, 0.0, -1e30).astype(jnp.float32)
        bias_rows.append(jnp.broadcast_to(bias, (BLK, tokens)))
    scores = scores + jnp.concatenate(bias_rows, axis=0)
    row_peak = jnp.max(scores, axis=1, keepdims=True)
    raised = jnp.exp(scores - row_peak)
    prob = raised / jnp.sum(raised, axis=1, keepdims=True)
    prob_b = prob.astype(jnp.bfloat16)
    ctx = jnp.dot(prob_b, v, preferred_element_type=jnp.float32).astype(jnp.bfloat16)
    ctx_ref[...] = ctx
    dprob = lax.dot_general(
        g, v, (((1,), (1,)), ((), ())), preferred_element_type=jnp.float32
    )
    row_dot = jnp.sum(
        g.astype(jnp.float32) * ctx.astype(jnp.float32), axis=1, keepdims=True
    )
    dscore = (prob * (dprob - row_dot)).astype(jnp.bfloat16)
    dq = jnp.dot(dscore, k, preferred_element_type=jnp.float32) * score_scale
    dq_ref[...] = dq.astype(jnp.bfloat16)
    dk_acc[...] += lax.dot_general(
        dscore, q, (((0,), (0,)), ((), ())), preferred_element_type=jnp.float32
    )
    dv_acc[...] += lax.dot_general(
        prob_b, g, (((0,), (0,)), ((), ())), preferred_element_type=jnp.float32
    )

    @pl.when(chunk == pl.num_programs(1) - 1)
    def _():
        dk_ref[...] = (dk_acc[...] * score_scale).astype(jnp.bfloat16)
        dv_ref[...] = dv_acc[...].astype(jnp.bfloat16)


def attention_call(index, queries, key_heads, value_heads, context_grad, random_blocks, results):
    heads_here = random_blocks.shape[0]
    tokens, width_here = queries.shape
    head_size = width_here // heads_here
    blocks = tokens // BLK
    chunks = tokens // ROWS
    group = 2 if heads_here % 2 == 0 else 1
    head0 = index * group
    rb_flat = random_blocks.reshape(-1)
    out_shape = jax.ShapeDtypeStruct((tokens, width_here), jnp.bfloat16)
    row_spec = pl.BlockSpec((ROWS, head_size), lambda h, c, rb: (c, h + head0))
    full_spec = pl.BlockSpec((tokens, head_size), lambda h, c, rb: (0, h + head0))
    aliased = results is not None
    extra = [pl.BlockSpec(memory_space=pl.ANY)] * 4 if aliased else []
    call = pl.pallas_call(
        functools.partial(attention_kernel, blocks, head_size, head0, aliased),
        out_shape=(out_shape, out_shape, out_shape, out_shape),
        grid_spec=pltpu.PrefetchScalarGridSpec(
            num_scalar_prefetch=1,
            grid=(group, chunks),
            in_specs=[row_spec, full_spec, full_spec, row_spec] + extra,
            out_specs=[row_spec, row_spec, full_spec, full_spec],
            scratch_shapes=[
                pltpu.VMEM((tokens, head_size), jnp.float32),
                pltpu.VMEM((tokens, head_size), jnp.float32),
            ],
        ),
        input_output_aliases={5: 0, 6: 1, 7: 2, 8: 3} if aliased else {},
        compiler_params=pltpu.CompilerParams(
            dimension_semantics=("arbitrary", "arbitrary"),
            vmem_limit_bytes=48 * 1024 * 1024,
        ),
        cost_estimate=pl.CostEstimate(
            flops=2 * tokens * tokens * head_size * 6 * group,
            transcendentals=tokens * tokens * group,
            bytes_accessed=7 * tokens * head_size * group * 2,
        ),
    )
    args = (rb_flat, queries, key_heads, value_heads, context_grad)
    return call(*args, *results) if aliased else call(*args)


def shift_over(block, axis, shift):
    count = lax.axis_size(axis)
    return lax.ppermute(block, axis, [(i, (i + shift) % count) for i in range(count)])


def wgrad_kernel(pieces, widths, part, offs_ref, *refs):
    groups = len(widths)
    piece_refs = refs[:pieces]
    ctx_refs = refs[pieces : pieces + 5 * groups]
    out_ref, acc, buf = refs[pieces + 5 * groups :]
    slot = pl.program_id(0)
    for k, piece_ref in enumerate(piece_refs):
        start = pl.multiple_of(offs_ref[k], 64)
        buf[pl.ds(start, piece_ref.shape[0]), :] = piece_ref[...]

    def term(cols, ctx):
        cols = cols[:, part[0] : part[0] + part[1]]
        return lax.dot_general(
            cols, ctx, (((0,), (0,)), ((), ())), preferred_element_type=jnp.float32
        )

    col0 = 0
    for g, width in enumerate(widths):
        own_ref, left_ref, far_lo_ref, far_hi_ref, right_ref = ctx_refs[5 * g : 5 * g + 5]
        half = far_lo_ref.shape[0]
        cols = slice(col0, col0 + width)

        @pl.when(slot == 0)
        def _():
            acc[:, cols] = term(buf[...], own_ref[...])

        @pl.when(slot == 1)
        def _():
            acc[:, cols] += term(buf[...], left_ref[...])

        @pl.when(slot == 2)
        def _():
            acc[:, cols] += term(buf[:half, :], far_lo_ref[...]) + term(
                buf[half:, :], far_hi_ref[...]
            )

        @pl.when(slot == 3)
        def _():
            out_ref[:, cols] = (acc[:, cols] + term(buf[...], right_ref[...])).astype(
                out_ref.dtype
            )

        col0 += width


def weight_block(piece_list, offsets, ctx_groups, part=None):
    slots = piece_list[0].shape[0]
    tokens = ctx_groups[0][0].shape[0]
    widths = tuple(group[0].shape[1] for group in ctx_groups)
    width = sum(widths)
    rows = piece_list[0].shape[2]
    part = (0, rows) if part is None else part
    piece_specs = [
        pl.BlockSpec((None, piece.shape[1], rows), lambda s, o: (s, 0, 0)) for piece in piece_list
    ]
    ctx_specs = []
    for group in ctx_groups:
        ctx_specs += [pl.BlockSpec(part.shape, lambda s, o: (0, 0)) for part in group]
    ctx_flat = [part for group in ctx_groups for part in group]
    return pl.pallas_call(
        functools.partial(wgrad_kernel, len(piece_list), widths, part),
        out_shape=jax.ShapeDtypeStruct((part[1], width), jnp.bfloat16),
        grid_spec=pltpu.PrefetchScalarGridSpec(
            num_scalar_prefetch=1,
            grid=(slots,),
            in_specs=piece_specs + ctx_specs,
            out_specs=pl.BlockSpec((part[1], width), lambda s, o: (0, 0)),
            scratch_shapes=[
                pltpu.VMEM((part[1], width), jnp.float32),
                pltpu.VMEM((tokens, rows), jnp.bfloat16),
            ],
        ),
        compiler_params=pltpu.CompilerParams(
            dimension_semantics=("arbitrary",), vmem_limit_bytes=48 * 1024 * 1024
        ),
        cost_estimate=pl.CostEstimate(
            flops=2 * slots * tokens * part[1] * width,
            transcendentals=0,
            bytes_accessed=2 * slots * tokens * (rows + width) + 2 * rows * width,
        ),
    )(offsets, *piece_list, *ctx_flat)


def ring_over_dp(ctx_rows):
    split = ctx_rows.shape[0] // 2
    from_left = shift_over(ctx_rows, "dp", 1)
    from_right = shift_over(ctx_rows, "dp", -1)
    far_lo = shift_over(from_left[:split], "dp", 1)
    far_hi = shift_over(from_right[split:], "dp", -1)
    return (ctx_rows, from_left, far_lo, far_hi, from_right)


def tensor_layout():
    count = lax.axis_size("tensor")
    along_y = 4 if count % 4 == 0 else count
    along_z = count // along_y
    return count, along_y, along_z


def yshift(x, k):
    count, along_y, _ = tensor_layout()
    route = [(t, (t // along_y) * along_y + (t % along_y + k) % along_y) for t in range(count)]
    return lax.ppermute(x, "tensor", route)


def zshift(x):
    count, along_y, along_z = tensor_layout()
    route = [(t, ((t // along_y + 1) % along_z) * along_y + t % along_y) for t in range(count)]
    return lax.ppermute(x, "tensor", route)


def gather_steps(block, last_over_z, between=lambda step, values: values):
    count, along_y, along_z = tensor_layout()
    pos = lax.axis_index("tensor")
    zl = pos // along_y
    y = pos % along_y
    rows = block.shape[1]
    split = rows // 2

    def place(dz, dy):
        return (((zl + dz) % along_z) * along_y + (y + dy) % along_y) * rows

    source = between(0, block)
    first = (zshift(source), yshift(source, 1), yshift(source, -1))
    z_piece, from_left, from_right = between(1, first)
    second = (
        yshift(z_piece, 1),
        yshift(z_piece, -1),
        yshift(from_left[:, :split], 1),
        yshift(from_right[:, split:], -1),
    )
    z_left, z_right, far_a, far_b = between(2, second)
    if last_over_z:
        third = (zshift(far_a), zshift(far_b))
    else:
        third = (yshift(z_left[:, :split], 1), yshift(z_right[:, split:], -1))
    pieces = [block, *first, *second, *third]
    offsets = [
        place(0, 0),
        place(1, 0),
        place(0, -1),
        place(0, 1),
        place(1, -1),
        place(1, 1),
        place(0, 2),
        place(0, 2) + split,
        place(1, 2),
        place(1, 2) + split,
    ]
    return pieces, jnp.stack(offsets).astype(jnp.int32)


def on_device(queries, key_heads, value_heads, context_grad, output_grad, random_blocks):
    dp_count = lax.axis_size("dp")
    dp_pos = lax.axis_index("dp")
    pipe_count = lax.axis_size("pipe")
    pipe_pos = lax.axis_index("pipe")
    upper_half = (pipe_pos >= pipe_count // 2).astype(jnp.int32)
    rows_here = output_grad.shape[2]
    width_model = output_grad.shape[3]
    quarter = width_model // (2 * dp_count)
    pieces = output_grad[0, 0].reshape(rows_here, 2, dp_count, quarter).transpose(2, 1, 0, 3)
    pieces = jnp.where(upper_half == 1, pieces, pieces[:, ::-1])
    received = [lax.dynamic_index_in_dim(pieces, dp_pos, 0, keepdims=False)]
    for shift in range(1, dp_count):
        target = (dp_pos + shift) % dp_count
        outgoing = lax.dynamic_index_in_dim(pieces, target, 0, keepdims=False)
        received.append(shift_over(outgoing, "dp", shift))
    moved = jnp.stack(received)
    attn_in = (queries[0, 0], key_heads[0, 0], value_heads[0, 0], context_grad[0, 0])
    calls = 3 if random_blocks.shape[0] % 6 == 0 else random_blocks.shape[0]
    state = {"results": None, "after": []}

    def between(step, values):
        if step < calls:
            state["results"] = attention_call(
                step, *attn_in, random_blocks, state["results"]
            )
            state["after"].append(state["results"])
        values, _ = lax.optimization_barrier((values, state["results"][1]))
        return values

    send_pieces, offsets = gather_steps(moved[:, 0], True, between)
    for index in range(3, calls):
        state["results"] = attention_call(index, *attn_in, random_blocks, state["results"])
    keep_pieces, _ = gather_steps(moved[:, 1], False)
    query_grad, ctx_rows, key_grad, value_grad = state["results"]
    early = state["after"][-2][1] if len(state["after"]) >= 2 else None
    if early is not None and ctx_rows.shape[1] % 3 == 0:
        cut = ctx_rows.shape[1] * 2 // 3
        ctx_groups = (ring_over_dp(early[:, :cut]), ring_over_dp(ctx_rows[:, cut:]))
    else:
        ctx_groups = (ring_over_dp(ctx_rows),)

    mirror = [(i, pipe_count - 1 - i) for i in range(pipe_count)]
    rows_out = send_pieces[0].shape[2]
    parts = ((0, rows_out // 2), (rows_out // 2, rows_out - rows_out // 2))
    incoming = jnp.concatenate(
        [
            lax.ppermute(weight_block(send_pieces, offsets, ctx_groups, part), "pipe", mirror)
            for part in parts
        ],
        axis=0,
    )
    keep_block = weight_block(keep_pieces, offsets, ctx_groups)
    weight_grad = (keep_block.astype(jnp.float32) + incoming.astype(jnp.float32)).astype(
        jnp.bfloat16
    )[None]
    shape4 = queries.shape
    return (
        query_grad.reshape(shape4),
        key_grad.reshape(shape4),
        value_grad.reshape(shape4),
        weight_grad,
    )


def solution(mesh):
    in_specs = (
        P("pipe", "dp", None, "tensor"),
        P("pipe", "dp", None, "tensor"),
        P("pipe", "dp", None, "tensor"),
        P("pipe", "dp", None, "tensor"),
        P("pipe", "dp", "tensor", None),
        P("tensor", None, None),
    )
    out_specs = (
        P("pipe", "dp", None, "tensor"),
        P("pipe", "dp", None, "tensor"),
        P("pipe", "dp", None, "tensor"),
        P("pipe", "dp", "tensor"),
    )
    return jax.shard_map(
        on_device, mesh=mesh, in_specs=in_specs, out_specs=out_specs, check_vma=False
    )
```

```python
import functools
import math

import jax
import jax.numpy as jnp
from jax import lax
from jax.experimental import pallas as pl
from jax.experimental.pallas import tpu as pltpu
from jax.sharding import PartitionSpec as P

BLK = 64
ROWS = 256


def attention_kernel(blocks, head_size, head0, aliased, rb_ref, q_ref, k_ref, v_ref, g_ref, *rest):
    if aliased:
        rest = rest[4:]
    dq_ref, ctx_ref, dk_ref, dv_ref, dk_acc, dv_acc = rest
    head = pl.program_id(0) + head0
    chunk = pl.program_id(1)
    score_scale = 1.0 / math.sqrt(head_size)
    tokens = k_ref.shape[0]
    per_chunk = q_ref.shape[0] // BLK
    mids = blocks - 2

    @pl.when(chunk == 0)
    def _():
        dk_acc[...] = jnp.zeros_like(dk_acc)
        dv_acc[...] = jnp.zeros_like(dv_acc)

    q = q_ref[...]
    k = k_ref[...]
    v = v_ref[...]
    g = g_ref[...]
    scores = lax.dot_general(
        q, k, (((1,), (1,)), ((), ())), preferred_element_type=jnp.float32
    ) * score_scale
    key_block = lax.broadcasted_iota(jnp.int32, (1, tokens), 1) // BLK
    bias_rows = []
    for i in range(per_chunk):
        qb = chunk * per_chunk + i
        row = jnp.clip(qb - 1, 0, mids - 1)
        base = (head * mids + row) * 3
        r1 = rb_ref[base]
        r2 = rb_ref[base + 1]
        r3 = rb_ref[base + 2]
        edge = jnp.logical_or(qb == 0, qb == blocks - 1)
        near = jnp.abs(key_block - qb) <= 1
        allowed = (
            (key_block == 0)
            | (key_block == blocks - 1)
            | near
            | (key_block == r1)
            | (key_block == r2)
            | (key_block == r3)
            | edge
        )
        bias = jnp.where(allowed, 0.0, -1e30).astype(jnp.float32)
        bias_rows.append(jnp.broadcast_to(bias, (BLK, tokens)))
    scores = scores + jnp.concatenate(bias_rows, axis=0)
    row_peak = jnp.max(scores, axis=1, keepdims=True)
    raised = jnp.exp(scores - row_peak)
    prob = raised / jnp.sum(raised, axis=1, keepdims=True)
    prob_b = prob.astype(jnp.bfloat16)
    ctx = jnp.dot(prob_b, v, preferred_element_type=jnp.float32).astype(jnp.bfloat16)
    ctx_ref[...] = ctx
    dprob = lax.dot_general(
        g, v, (((1,), (1,)), ((), ())), preferred_element_type=jnp.float32
    )
    row_dot = jnp.sum(
        g.astype(jnp.float32) * ctx.astype(jnp.float32), axis=1, keepdims=True
    )
    dscore = (prob * (dprob - row_dot)).astype(jnp.bfloat16)
    dq = jnp.dot(dscore, k, preferred_element_type=jnp.float32) * score_scale
    dq_ref[...] = dq.astype(jnp.bfloat16)
    dk_acc[...] += lax.dot_general(
        dscore, q, (((0,), (0,)), ((), ())), preferred_element_type=jnp.float32
    )
    dv_acc[...] += lax.dot_general(
        prob_b, g, (((0,), (0,)), ((), ())), preferred_element_type=jnp.float32
    )

    @pl.when(chunk == pl.num_programs(1) - 1)
    def _():
        dk_ref[...] = (dk_acc[...] * score_scale).astype(jnp.bfloat16)
        dv_ref[...] = dv_acc[...].astype(jnp.bfloat16)


def attention_call(index, queries, key_heads, value_heads, context_grad, random_blocks, results):
    heads_here = random_blocks.shape[0]
    tokens, width_here = queries.shape
    head_size = width_here // heads_here
    blocks = tokens // BLK
    chunks = tokens // ROWS
    group = 2 if heads_here % 2 == 0 else 1
    head0 = index * group
    rb_flat = random_blocks.reshape(-1)
    out_shape = jax.ShapeDtypeStruct((tokens, width_here), jnp.bfloat16)
    row_spec = pl.BlockSpec((ROWS, head_size), lambda h, c, rb: (c, h + head0))
    full_spec = pl.BlockSpec((tokens, head_size), lambda h, c, rb: (0, h + head0))
    aliased = results is not None
    extra = [pl.BlockSpec(memory_space=pl.ANY)] * 4 if aliased else []
    call = pl.pallas_call(
        functools.partial(attention_kernel, blocks, head_size, head0, aliased),
        out_shape=(out_shape, out_shape, out_shape, out_shape),
        grid_spec=pltpu.PrefetchScalarGridSpec(
            num_scalar_prefetch=1,
            grid=(group, chunks),
            in_specs=[row_spec, full_spec, full_spec, row_spec] + extra,
            out_specs=[row_spec, row_spec, full_spec, full_spec],
            scratch_shapes=[
                pltpu.VMEM((tokens, head_size), jnp.float32),
                pltpu.VMEM((tokens, head_size), jnp.float32),
            ],
        ),
        input_output_aliases={5: 0, 6: 1, 7: 2, 8: 3} if aliased else {},
        compiler_params=pltpu.CompilerParams(
            dimension_semantics=("arbitrary", "arbitrary"),
            vmem_limit_bytes=48 * 1024 * 1024,
        ),
        cost_estimate=pl.CostEstimate(
            flops=2 * tokens * tokens * head_size * 6 * group,
            transcendentals=tokens * tokens * group,
            bytes_accessed=7 * tokens * head_size * group * 2,
        ),
    )
    args = (rb_flat, queries, key_heads, value_heads, context_grad)
    return call(*args, *results) if aliased else call(*args)


def shift_over(block, axis, shift):
    count = lax.axis_size(axis)
    return lax.ppermute(block, axis, [(i, (i + shift) % count) for i in range(count)])


def wgrad_kernel(pieces, widths, part, offs_ref, *refs):
    groups = len(widths)
    piece_refs = refs[:pieces]
    ctx_refs = refs[pieces : pieces + 5 * groups]
    out_ref, acc, buf = refs[pieces + 5 * groups :]
    slot = pl.program_id(0)
    for k, piece_ref in enumerate(piece_refs):
        start = pl.multiple_of(offs_ref[k], 64)
        buf[pl.ds(start, piece_ref.shape[0]), :] = piece_ref[...]

    def term(cols, ctx):
        cols = cols[:, part[0] : part[0] + part[1]]
        return lax.dot_general(
            cols, ctx, (((0,), (0,)), ((), ())), preferred_element_type=jnp.float32
        )

    col0 = 0
    for g, width in enumerate(widths):
        own_ref, left_ref, far_lo_ref, far_hi_ref, right_ref = ctx_refs[5 * g : 5 * g + 5]
        half = far_lo_ref.shape[0]
        cols = slice(col0, col0 + width)

        @pl.when(slot == 0)
        def _():
            acc[:, cols] = term(buf[...], own_ref[...])

        @pl.when(slot == 1)
        def _():
            acc[:, cols] += term(buf[...], left_ref[...])

        @pl.when(slot == 2)
        def _():
            acc[:, cols] += term(buf[:half, :], far_lo_ref[...]) + term(
                buf[half:, :], far_hi_ref[...]
            )

        @pl.when(slot == 3)
        def _():
            out_ref[:, cols] = (acc[:, cols] + term(buf[...], right_ref[...])).astype(
                out_ref.dtype
            )

        col0 += width


def weight_block(piece_list, offsets, ctx_groups, part=None):
    slots = piece_list[0].shape[0]
    tokens = ctx_groups[0][0].shape[0]
    widths = tuple(group[0].shape[1] for group in ctx_groups)
    width = sum(widths)
    rows = piece_list[0].shape[2]
    part = (0, rows) if part is None else part
    piece_specs = [
        pl.BlockSpec((None, piece.shape[1], rows), lambda s, o: (s, 0, 0)) for piece in piece_list
    ]
    ctx_specs = []
    for group in ctx_groups:
        ctx_specs += [pl.BlockSpec(part.shape, lambda s, o: (0, 0)) for part in group]
    ctx_flat = [part for group in ctx_groups for part in group]
    return pl.pallas_call(
        functools.partial(wgrad_kernel, len(piece_list), widths, part),
        out_shape=jax.ShapeDtypeStruct((part[1], width), jnp.bfloat16),
        grid_spec=pltpu.PrefetchScalarGridSpec(
            num_scalar_prefetch=1,
            grid=(slots,),
            in_specs=piece_specs + ctx_specs,
            out_specs=pl.BlockSpec((part[1], width), lambda s, o: (0, 0)),
            scratch_shapes=[
                pltpu.VMEM((part[1], width), jnp.float32),
                pltpu.VMEM((tokens, rows), jnp.bfloat16),
            ],
        ),
        compiler_params=pltpu.CompilerParams(
            dimension_semantics=("arbitrary",), vmem_limit_bytes=48 * 1024 * 1024
        ),
        cost_estimate=pl.CostEstimate(
            flops=2 * slots * tokens * part[1] * width,
            transcendentals=0,
            bytes_accessed=2 * slots * tokens * (rows + width) + 2 * rows * width,
        ),
    )(offsets, *piece_list, *ctx_flat)


def ring_over_dp(ctx_rows):
    split = ctx_rows.shape[0] // 2
    from_left = shift_over(ctx_rows, "dp", 1)
    from_right = shift_over(ctx_rows, "dp", -1)
    far_lo = shift_over(from_left[:split], "dp", 1)
    far_hi = shift_over(from_right[split:], "dp", -1)
    return (ctx_rows, from_left, far_lo, far_hi, from_right)


def tensor_layout():
    count = lax.axis_size("tensor")
    along_y = 4 if count % 4 == 0 else count
    along_z = count // along_y
    return count, along_y, along_z


def yshift(x, k):
    count, along_y, _ = tensor_layout()
    route = [(t, (t // along_y) * along_y + (t % along_y + k) % along_y) for t in range(count)]
    return lax.ppermute(x, "tensor", route)


def zshift(x):
    count, along_y, along_z = tensor_layout()
    route = [(t, ((t // along_y + 1) % along_z) * along_y + t % along_y) for t in range(count)]
    return lax.ppermute(x, "tensor", route)


def gather_steps(block, last_over_z, between=lambda step, values: values):
    count, along_y, along_z = tensor_layout()
    pos = lax.axis_index("tensor")
    zl = pos // along_y
    y = pos % along_y
    rows = block.shape[1]
    split = rows // 2

    def place(dz, dy):
        return (((zl + dz) % along_z) * along_y + (y + dy) % along_y) * rows

    source = between(0, block)
    first = (zshift(source), yshift(source, 1), yshift(source, -1))
    z_piece, from_left, from_right = between(1, first)
    second = (
        yshift(z_piece, 1),
        yshift(z_piece, -1),
        yshift(from_left[:, :split], 1),
        yshift(from_right[:, split:], -1),
    )
    z_left, z_right, far_a, far_b = between(2, second)
    if last_over_z:
        third = (zshift(far_a), zshift(far_b))
    else:
        third = (yshift(z_left[:, :split], 1), yshift(z_right[:, split:], -1))
    pieces = [block, *first, *second, *third]
    offsets = [
        place(0, 0),
        place(1, 0),
        place(0, -1),
        place(0, 1),
        place(1, -1),
        place(1, 1),
        place(0, 2),
        place(0, 2) + split,
        place(1, 2),
        place(1, 2) + split,
    ]
    return pieces, jnp.stack(offsets).astype(jnp.int32)


def on_device(queries, key_heads, value_heads, context_grad, output_grad, random_blocks):
    dp_count = lax.axis_size("dp")
    dp_pos = lax.axis_index("dp")
    pipe_count = lax.axis_size("pipe")
    pipe_pos = lax.axis_index("pipe")
    upper_half = (pipe_pos >= pipe_count // 2).astype(jnp.int32)
    rows_here = output_grad.shape[2]
    width_model = output_grad.shape[3]
    quarter = width_model // (2 * dp_count)
    pieces = output_grad[0, 0].reshape(rows_here, 2, dp_count, quarter).transpose(2, 1, 0, 3)
    pieces = jnp.where(upper_half == 1, pieces, pieces[:, ::-1])
    received = [lax.dynamic_index_in_dim(pieces, dp_pos, 0, keepdims=False)]
    for shift in range(1, dp_count):
        target = (dp_pos + shift) % dp_count
        outgoing = lax.dynamic_index_in_dim(pieces, target, 0, keepdims=False)
        received.append(shift_over(outgoing, "dp", shift))
    moved = jnp.stack(received)
    attn_in = (queries[0, 0], key_heads[0, 0], value_heads[0, 0], context_grad[0, 0])
    calls = 3 if random_blocks.shape[0] % 6 == 0 else random_blocks.shape[0]
    state = {"results": None, "after": []}

    def between(step, values):
        if step < calls:
            state["results"] = attention_call(
                step, *attn_in, random_blocks, state["results"]
            )
            state["after"].append(state["results"])
        values, _ = lax.optimization_barrier((values, state["results"][1]))
        return values

    send_pieces, offsets = gather_steps(moved[:, 0], True, between)
    for index in range(3, calls):
        state["results"] = attention_call(index, *attn_in, random_blocks, state["results"])
    keep_pieces, _ = gather_steps(moved[:, 1], False)
    query_grad, ctx_rows, key_grad, value_grad = state["results"]
    early = state["after"][-2][1] if len(state["after"]) >= 2 else None
    if early is not None and ctx_rows.shape[1] % 3 == 0:
        cut = ctx_rows.shape[1] * 2 // 3
        ctx_groups = (ring_over_dp(early[:, :cut]), ring_over_dp(ctx_rows[:, cut:]))
    else:
        ctx_groups = (ring_over_dp(ctx_rows),)

    mirror = [(i, pipe_count - 1 - i) for i in range(pipe_count)]
    rows_out = send_pieces[0].shape[2]
    count = 3 if rows_out % 384 == 0 else 2
    step = rows_out // count
    parts = tuple((i * step, step) for i in range(count))
    incoming = jnp.concatenate(
        [
            lax.ppermute(weight_block(send_pieces, offsets, ctx_groups, part), "pipe", mirror)
            for part in parts
        ],
        axis=0,
    )
    keep_block = weight_block(keep_pieces, offsets, ctx_groups)
    weight_grad = (keep_block.astype(jnp.float32) + incoming.astype(jnp.float32)).astype(
        jnp.bfloat16
    )[None]
    shape4 = queries.shape
    return (
        query_grad.reshape(shape4),
        key_grad.reshape(shape4),
        value_grad.reshape(shape4),
        weight_grad,
    )


def solution(mesh):
    in_specs = (
        P("pipe", "dp", None, "tensor"),
        P("pipe", "dp", None, "tensor"),
        P("pipe", "dp", None, "tensor"),
        P("pipe", "dp", None, "tensor"),
        P("pipe", "dp", "tensor", None),
        P("tensor", None, None),
    )
    out_specs = (
        P("pipe", "dp", None, "tensor"),
        P("pipe", "dp", None, "tensor"),
        P("pipe", "dp", None, "tensor"),
        P("pipe", "dp", "tensor"),
    )
    return jax.shard_map(
        on_device, mesh=mesh, in_specs=in_specs, out_specs=out_specs, check_vma=False
    )
```
